256 devices in a mesh: roll: 32 (over y, z_lo, core), seq: 8 (over x, z_hi).
Axes of the slice: x: 4, y: 4, z: 8 (z_hi: 2, z_lo: 4; z = z_hi * 4 + z_lo), core: 2. Of those that a mesh axis runs over, the one named last changes fastest.
Arguments:
- queries: bfloat16 [65536, 3072], P(('roll', 'seq')), parts along dimension 0, may hold values from -7.5 to 7.5
- keys_in: bfloat16 [65536, 3072], P(('roll', 'seq')), parts along dimension 0, may hold values from -7.5 to 7.5
- values_in: bfloat16 [65536, 3072], P(('roll', 'seq')), parts along dimension 0, may hold values from -6 to 6
- latent_proj: bfloat16 [3072, 64], replicated, may hold values from -3 to 3
- conv_weight: bfloat16 [432, 512], replicated, may hold values from -0.3125 to 0.3125
- conv_bias: float32 [512], replicated, may hold values from -3 to 3
- pool_weight: float32 [8, 2, 8, 64], P('seq'), may hold values from -5 to 5
- tile_block: int32 [1024], P('roll'), parts along dimension 0, may hold values from 0 to 31, each once
- owner_slot: int32 [512], P('roll'), parts along dimension 0, may hold values from 0 to 15, each once
Outputs:
- decoded: bfloat16 [256, 2, 8, 64, 512], P(('roll', 'seq')), parts along dimension 0
- policy_features: float32 [512, 512], P(('roll', 'seq')), parts along dimension 0
The draws below stay inside these ranges and needn't reach their ends.
There are 32 independent parts, one for each index of `roll`. The reference program is written for one: setup_inputs(seed, part) draws one part's arguments, and reference() takes and returns one part's arrays. A program takes and returns all parts, laid end to end along the dimension named above; an argument that names none is the same for every part. Nothing has to cross between parts.
Inputs may be any that keep to these rules, and one draw needn't show every extreme that they name: `tile_block`: each piece index once. `owner_slot`: each row once.
All inputs are finite; a program needn't handle non-finite values.
Results may differ from the reference program's by a relative error of at most 0.013.
Values may be sent and summed in bfloat16 or wider, within the bound.
No kernel may reach another device: no remote copies, remote signals or barrier semaphores. Data moves between devices by JAX's collectives and lax.ppermute only.
A program may use at most 64 MiB of HBM per device.

```python
import math
import jax
import jax.numpy as jnp
from jax import lax

H = 24
HD = 128
LC = 16
CO = 512
S_DEV = 256
RT = 4
WT = 32
TR = 2
FT = 2
RL = 8
COLS = 64
TILES = 8
PIECES = 32
TF = 4
SEQ = 2048
FRAMES = 8
ROWS = 16
NB = 16
VB = 512
KC = 432


def draw_queries(key, part):
    base = jnp.clip(jax.random.normal(jax.random.fold_in(key, 11), (SEQ, H * HD), jnp.float32), -4.0, 4.0)
    return base.astype(jnp.bfloat16)


def draw_keys_in(key, part):
    base = jnp.clip(jax.random.normal(jax.random.fold_in(key, 21), (SEQ, H * HD), jnp.float32), -4.0, 4.0)
    return base.astype(jnp.bfloat16)


def levels(rng, extent, cuts, least, high):
    level, own = 1.0, jax.random.fold_in(rng, 6)
    for axis_at, blocks in cuts:
        steps = jnp.exp(jax.random.uniform(jax.random.fold_in(own, axis_at), (blocks,), jnp.float32, least / len(cuts), high / len(cuts)))
        level = level * jnp.repeat(steps, extent[axis_at] // blocks).reshape([-1 if axis == axis_at else 1 for axis in range(len(extent))])
    return level


def normal_values(own_key, dims, width, reach, split=(), kind=jnp.bfloat16):
    level = levels(own_key, dims, split, -0.22, 0.18) if split else 1.0
    values = jax.random.normal(own_key, dims, jnp.float32) * width * level
    return jnp.minimum(jnp.maximum(values, -reach), reach).astype(kind)


def setup_inputs(seed: int = 0, part: int = 0) -> dict:
    splits = jax.random.split(jax.random.key(seed), 10)
    own_keys = jax.random.split(jax.random.fold_in(splits[9], part), 10)
    return {
        "queries": draw_queries(jax.random.fold_in(jax.random.fold_in(splits[9], part), 71), part),
        "keys_in": draw_keys_in(jax.random.fold_in(jax.random.fold_in(splits[9], part), 71), part),
        "values_in": normal_values(own_keys[2], (SEQ, H * HD), 1.0, 6.0, ((0, 8),)),
        "latent_proj": normal_values(splits[3], (H * HD, 4 * LC), 0.5, 3.0),
        "conv_weight": normal_values(splits[4], (KC, CO), KC ** -0.5, 0.3125),
        "conv_bias": normal_values(splits[5], (CO,), 0.5, 3.0, (), jnp.float32),
        "pool_weight": normal_values(splits[6], (TILES, FT, RL, COLS), 1.0, 5.0, ((0, 8),), jnp.float32),
        "tile_block": jax.random.permutation(own_keys[7], PIECES).astype(jnp.int32),
        "owner_slot": jax.random.permutation(own_keys[8], NB).astype(jnp.int32),
    }


def head_attention(inputs):
    query_head, key_head, value_head = inputs
    scores = jnp.dot(query_head, key_head.T, preferred_element_type=jnp.float32) * (1.0 / math.sqrt(HD))
    expo = jnp.exp(scores - lax.optimization_barrier(jnp.max(scores, axis=-1, keepdims=True)))
    totals = lax.optimization_barrier(jnp.sum(expo, axis=-1, keepdims=True))
    mixed = jnp.dot(expo.astype(jnp.bfloat16), value_head, preferred_element_type=jnp.float32)
    return (mixed / totals).astype(jnp.bfloat16)

def window_columns(volume):
    frame_count = volume.shape[0] - 2
    row_count = volume.shape[1] - 2
    col_count = volume.shape[2] - 2
    pieces = [volume[a:a + frame_count, b:b + row_count, c:c + col_count] for a in range(3) for b in range(3) for c in range(3)]
    return jnp.concatenate(pieces, axis=-1).reshape(frame_count * row_count * col_count, 27 * volume.shape[3])

def split_heads(matrix):
    return matrix.reshape(SEQ, H, HD).transpose(1, 0, 2)

def reference(queries, keys_in, values_in, latent_proj, conv_weight, conv_bias, pool_weight, tile_block, owner_slot):
    heads_out = lax.map(head_attention, (split_heads(queries), split_heads(keys_in), split_heads(values_in)))
    attn_out = heads_out.transpose(1, 0, 2).reshape(SEQ, H * HD)
    latent_tokens = jnp.dot(attn_out, latent_proj, preferred_element_type=jnp.float32).astype(jnp.bfloat16)
    blocks = latent_tokens.reshape(PIECES, S_DEV // 4, 4 * LC)[tile_block]
    blocks = blocks.reshape(TF, TR, FT, RT, WT, 2, 2, LC).transpose(0, 2, 1, 3, 5, 4, 6, 7)
    video = blocks.reshape(FRAMES, ROWS, COLS, LC)
    volume = jnp.pad(video, ((2, 0), (1, 1), (1, 1), (0, 0)))
    pre_act = jnp.dot(window_columns(volume), conv_weight, preferred_element_type=jnp.float32) + conv_bias
    pre_tiles = pre_act.reshape(TF, FT, TR, RL, COLS, CO).transpose(0, 2, 1, 3, 4, 5).reshape(TILES, FT, RL, COLS, CO)
    decoded = pre_tiles.astype(jnp.bfloat16)
    weighted = jax.nn.silu(pre_tiles) * pool_weight[..., None]
    pooled = lax.optimization_barrier(jnp.sum(weighted, axis=(0, 1, 2))).reshape(NB, COLS // NB, CO).sum(axis=1) / math.sqrt(VB)
    policy = jnp.zeros((NB, CO), jnp.float32).at[owner_slot].set(pooled)
    return (decoded, policy)
```

```python
import math

import jax
import jax.numpy as jnp
from jax import lax
from jax.sharding import PartitionSpec as P

H = 24
HD = 128
LC = 16
CO = 512
S_DEV = 256
RT = 4
WT = 32
TR = 2
BPD = 2
FT = 2
RL = 8
COLS = 64
QUERY_BLOCK = 512


def shifted(array, axis, by):
    length = lax.axis_size(axis)
    pairs = [(i, i + by) for i in range(length) if 0 <= i + by < length]
    return lax.ppermute(array, axis, pairs)


def swapped(array, axis, bit):
    return lax.ppermute(array, axis, [(i, i ^ 1 << bit) for i in range(lax.axis_size(axis))])


def butterfly_sum(array, axis):
    length = lax.axis_size(axis)
    bit = 0
    while (1 << bit) < length:
        array = array + swapped(array, axis, bit)
        bit += 1
    return array


def head_attention(query, key, value):
    length = query.shape[0]
    score_scale = 1.0 / math.sqrt(query.shape[1])
    query_blocks = query.reshape(length // QUERY_BLOCK, QUERY_BLOCK, query.shape[1])

    def one_block(query_part):
        scores = jnp.dot(query_part, key.T, preferred_element_type=jnp.float32) * score_scale
        expo = jnp.exp(scores - jnp.max(scores, axis=-1, keepdims=True))
        totals = jnp.sum(expo, axis=-1, keepdims=True)
        mixed = jnp.dot(expo.astype(jnp.bfloat16), value, preferred_element_type=jnp.float32)
        return (mixed / totals).astype(jnp.bfloat16)

    return lax.map(one_block, query_blocks).reshape(length, query.shape[1])


def window_columns(volume):
    frame_count = volume.shape[0] - 2
    row_count = volume.shape[1] - 2
    col_count = volume.shape[2] - 2
    pieces = [
        volume[a : a + frame_count, b : b + row_count, c : c + col_count]
        for a in range(3)
        for b in range(3)
        for c in range(3)
    ]
    return jnp.concatenate(pieces, axis=-1).reshape(
        frame_count * row_count * col_count, 27 * volume.shape[3]
    )


def local(
    queries,
    keys_in,
    values_in,
    latent_proj,
    conv_weight,
    conv_bias,
    pool_weight,
    tile_block,
    owner_slot,
):
    group_count = lax.axis_size("seq")
    my_index = lax.axis_index("seq")
    seq_len = S_DEV * group_count
    heads_dev = H // group_count
    quarter = S_DEV // 4

    def to_groups(matrix):
        return matrix.reshape(S_DEV, group_count, heads_dev, HD)

    q_groups, k_groups, v_groups = to_groups(queries), to_groups(keys_in), to_groups(values_in)
    partial = None
    for slot in range(heads_dev):
        stacked = jnp.stack(
            [q_groups[:, :, slot], k_groups[:, :, slot], v_groups[:, :, slot]], axis=2
        )
        gathered = lax.all_to_all(stacked, "seq", split_axis=1, concat_axis=0, tiled=True)
        head_out = head_attention(gathered[:, 0, 0], gathered[:, 0, 1], gathered[:, 0, 2])
        proj_rows = lax.dynamic_slice_in_dim(latent_proj, (my_index * heads_dev + slot) * HD, HD, 0)
        term = jnp.dot(head_out, proj_rows, preferred_element_type=jnp.float32)
        partial = term if partial is None else partial + term

    ordered = partial.reshape(4 * group_count, quarter, 4 * LC)[tile_block]
    ordered = ordered.reshape(group_count, S_DEV, 4 * LC)
    returned = lax.all_to_all(ordered, "seq", split_axis=0, concat_axis=0, tiled=True)
    latent = jnp.sum(returned, axis=0).astype(jnp.bfloat16)
    tile_latent = (
        latent.reshape(FT, RT, WT, 2, 2, LC).transpose(0, 1, 3, 2, 4, 5).reshape(FT, RL, COLS * LC)
    )
    earlier = shifted(tile_latent, "seq", TR)
    extended = jnp.concatenate([earlier, tile_latent], axis=0)
    band_row = my_index % TR
    upper_band = band_row == 0
    outgoing = jnp.where(upper_band, extended[:, RL - 1 :], extended[:, :1])
    incoming = swapped(outgoing, "seq", 0)
    above = jnp.where(upper_band, jnp.zeros_like(incoming), incoming)
    below = jnp.where(upper_band, incoming, jnp.zeros_like(incoming))
    volume = jnp.concatenate([above, extended, below], axis=1).reshape(FT + 2, RL + 2, COLS, LC)
    volume = jnp.pad(volume, ((0, 0), (0, 0), (1, 1), (0, 0)))
    pre_act = (
        jnp.dot(window_columns(volume), conv_weight, preferred_element_type=jnp.float32) + conv_bias
    )
    decoded = pre_act.astype(jnp.bfloat16).reshape(1, FT, RL, COLS, CO)
    block_count = BPD * group_count
    band_voxels = group_count // TR * FT * TR * RL * (COLS // block_count)
    weighted = jax.nn.silu(pre_act).reshape(FT, RL, COLS, CO) * pool_weight[0][..., None]
    pooled_term = jnp.sum(weighted, axis=(0, 1)).reshape(block_count, COLS // block_count, CO).sum(
        axis=1
    ) / math.sqrt(band_voxels)
    total_pooled = butterfly_sum(pooled_term, "seq")
    wanted_rows = my_index * BPD + jnp.arange(BPD, dtype=jnp.int32)
    chooser = (owner_slot[None, :] == wanted_rows[:, None]).astype(jnp.float32)
    policy = jnp.dot(
        chooser, total_pooled, precision=lax.Precision.HIGHEST, preferred_element_type=jnp.float32
    )
    return (decoded, policy)


def solution(mesh):
    placed = (
        P(("roll", "seq"), None),
        P(("roll", "seq"), None),
        P(("roll", "seq"), None),
        P(),
        P(),
        P(),
        P("seq", None, None, None),
        P("roll"),
        P("roll"),
    )
    return jax.shard_map(
        local,
        mesh=mesh,
        in_specs=placed,
        out_specs=(P(("roll", "seq"), None, None, None, None), P(("roll", "seq"), None)),
        check_vma=False,
    )
```

```python
import math

import jax
import jax.numpy as jnp
from jax import lax
from jax.sharding import PartitionSpec as P

H = 24
HD = 128
LC = 16
CO = 512
S_DEV = 256
RT = 4
WT = 32
TR = 2
BPD = 2
FT = 2
RL = 8
COLS = 64
QUERY_BLOCK = 512


def shifted(array, axis, by):
    length = lax.axis_size(axis)
    pairs = [(i, i + by) for i in range(length) if 0 <= i + by < length]
    return lax.ppermute(array, axis, pairs)


def swapped(array, axis, bit):
    return lax.ppermute(array, axis, [(i, i ^ 1 << bit) for i in range(lax.axis_size(axis))])


def butterfly_sum(array, axis):
    length = lax.axis_size(axis)
    bit = 0
    while (1 << bit) < length:
        array = array + swapped(array, axis, bit)
        bit += 1
    return array


def exchange_sum(blocks, axis, my_index):
    length = lax.axis_size(axis)
    total = lax.dynamic_index_in_dim(blocks, my_index, 0, keepdims=False)
    for step in range(1, length):
        piece = lax.dynamic_index_in_dim(blocks, (my_index + step) % length, 0, keepdims=False)
        total = total + lax.ppermute(
            piece, axis, [(i, (i + step) % length) for i in range(length)]
        )
    return total


def head_attention(query, key, value):
    length = query.shape[0]
    score_scale = 1.0 / math.sqrt(query.shape[1])
    query_blocks = query.reshape(length // QUERY_BLOCK, QUERY_BLOCK, query.shape[1])

    def one_block(query_part):
        scores = jnp.dot(query_part, key.T, preferred_element_type=jnp.float32) * score_scale
        expo = jnp.exp(scores - jnp.max(scores, axis=-1, keepdims=True))
        totals = jnp.sum(expo, axis=-1, keepdims=True)
        mixed = jnp.dot(expo.astype(jnp.bfloat16), value, preferred_element_type=jnp.float32)
        return (mixed / totals).astype(jnp.bfloat16)

    return lax.map(one_block, query_blocks).reshape(length, query.shape[1])


def window_columns(volume):
    frame_count = volume.shape[0] - 2
    row_count = volume.shape[1] - 2
    col_count = volume.shape[2] - 2
    pieces = [
        volume[a : a + frame_count, b : b + row_count, c : c + col_count]
        for a in range(3)
        for b in range(3)
        for c in range(3)
    ]
    return jnp.concatenate(pieces, axis=-1).reshape(
        frame_count * row_count * col_count, 27 * volume.shape[3]
    )


def local(
    queries,
    keys_in,
    values_in,
    latent_proj,
    conv_weight,
    conv_bias,
    pool_weight,
    tile_block,
    owner_slot,
):
    group_count = lax.axis_size("seq")
    my_index = lax.axis_index("seq")
    seq_len = S_DEV * group_count
    heads_dev = H // group_count
    quarter = S_DEV // 4

    def to_groups(matrix):
        return matrix.reshape(S_DEV, group_count, heads_dev, HD)

    q_groups, k_groups, v_groups = to_groups(queries), to_groups(keys_in), to_groups(values_in)
    partial = None
    for slot in range(heads_dev):
        stacked = jnp.stack(
            [q_groups[:, :, slot], k_groups[:, :, slot], v_groups[:, :, slot]], axis=2
        )
        gathered = lax.all_to_all(stacked, "seq", split_axis=1, concat_axis=0, tiled=True)
        head_out = head_attention(gathered[:, 0, 0], gathered[:, 0, 1], gathered[:, 0, 2])
        proj_rows = lax.dynamic_slice_in_dim(latent_proj, (my_index * heads_dev + slot) * HD, HD, 0)
        term = jnp.dot(head_out, proj_rows, preferred_element_type=jnp.float32)
        partial = term if partial is None else partial + term

    ordered = partial.reshape(4 * group_count, quarter, 4 * LC)[tile_block]
    ordered = ordered.reshape(group_count, S_DEV, 4 * LC)
    latent = exchange_sum(ordered, "seq", my_index).astype(jnp.bfloat16)
    tile_latent = (
        latent.reshape(FT, RT, WT, 2, 2, LC).transpose(0, 1, 3, 2, 4, 5).reshape(FT, RL, COLS * LC)
    )
    band_row = my_index % TR
    upper_band = band_row == 0
    outgoing = jnp.where(upper_band, tile_latent[:, RL - 1 :], tile_latent[:, :1])
    earlier = shifted(tile_latent, "seq", TR)
    beside = swapped(outgoing, "seq", 0)
    diagonal = lax.ppermute(
        outgoing,
        "seq",
        [(i, (i ^ 1) + TR) for i in range(group_count) if (i ^ 1) + TR < group_count],
    )
    extended = jnp.concatenate([earlier, tile_latent], axis=0)
    incoming = jnp.concatenate([diagonal, beside], axis=0)
    above = jnp.where(upper_band, jnp.zeros_like(incoming), incoming)
    below = jnp.where(upper_band, incoming, jnp.zeros_like(incoming))
    volume = jnp.concatenate([above, extended, below], axis=1).reshape(FT + 2, RL + 2, COLS, LC)
    volume = jnp.pad(volume, ((0, 0), (0, 0), (1, 1), (0, 0)))
    kernel = conv_weight.reshape(3, 3, 3, LC, CO)
    pre_act = lax.conv_general_dilated(
        volume[None],
        kernel,
        window_strides=(1, 1, 1),
        padding="VALID",
        dimension_numbers=("NDHWC", "DHWIO", "NDHWC"),
        preferred_element_type=jnp.float32,
    )[0] + conv_bias
    decoded = pre_act.astype(jnp.bfloat16).reshape(1, FT, RL, COLS, CO)
    block_count = BPD * group_count
    band_voxels = group_count // TR * FT * TR * RL * (COLS // block_count)
    weighted = jax.nn.silu(pre_act).reshape(FT, RL, COLS, CO) * pool_weight[0][..., None]
    pooled_term = jnp.sum(weighted, axis=(0, 1)).reshape(block_count, COLS // block_count, CO).sum(
        axis=1
    ) / math.sqrt(band_voxels)
    slots = jnp.arange(block_count, dtype=jnp.int32)
    chooser = (owner_slot[None, :] == slots[:, None]).astype(jnp.float32)
    by_owner = jnp.dot(
        chooser, pooled_term, precision=lax.Precision.HIGHEST, preferred_element_type=jnp.float32
    )
    policy = exchange_sum(by_owner.reshape(group_count, BPD, CO), "seq", my_index)
    return (decoded, policy)


def solution(mesh):
    placed = (
        P(("roll", "seq"), None),
        P(("roll", "seq"), None),
        P(("roll", "seq"), None),
        P(),
        P(),
        P(),
        P("seq", None, None, None),
        P("roll"),
        P("roll"),
    )
    return jax.shard_map(
        local,
        mesh=mesh,
        in_specs=placed,
        out_specs=(P(("roll", "seq"), None, None, None, None), P(("roll", "seq"), None)),
        check_vma=False,
    )
```

```python
import math

import jax
import numpy as np
import jax.numpy as jnp
from jax import lax
from jax.sharding import PartitionSpec as P

H = 24
HD = 128
LC = 16
CO = 512
S_DEV = 256
RT = 4
WT = 32
TR = 2
BPD = 2
FT = 2
RL = 8
COLS = 64
QUERY_BLOCK = 512


def shifted(array, axis, by):
    length = lax.axis_size(axis)
    pairs = [(i, i + by) for i in range(length) if 0 <= i + by < length]
    return lax.ppermute(array, axis, pairs)


def swapped(array, axis, bit):
    return lax.ppermute(array, axis, [(i, i ^ 1 << bit) for i in range(lax.axis_size(axis))])


def butterfly_sum(array, axis):
    length = lax.axis_size(axis)
    bit = 0
    while (1 << bit) < length:
        array = array + swapped(array, axis, bit)
        bit += 1
    return array


def halo_tables(tile_count):
    quarter = S_DEV // 4
    tile_token = np.arange(S_DEV)
    positions, offsets = [], []
    for tile in range(tile_count):
        band = tile % TR
        token_row = 0 if band == 0 else RT - 1
        row_tokens = np.array(
            [f * RT * WT + token_row * WT + c for f in range(FT) for c in range(WT)]
        )
        earlier = tile - TR if tile >= TR else 0
        diagonal = (tile - TR) ^ 1 if tile >= TR else 0
        parts = [(earlier, tile_token), (tile, tile_token), (diagonal, row_tokens), (tile ^ 1, row_tokens)]
        positions.append(np.concatenate([4 * src + idx // quarter for src, idx in parts]))
        offsets.append(np.concatenate([idx % quarter for src, idx in parts]))
    return np.stack(positions).astype(np.int32), np.stack(offsets).astype(np.int32)


def exchange_sum(blocks, axis, my_index):
    length = lax.axis_size(axis)
    total = lax.dynamic_index_in_dim(blocks, my_index, 0, keepdims=False)
    for step in range(1, length):
        piece = lax.dynamic_index_in_dim(blocks, (my_index + step) % length, 0, keepdims=False)
        total = total + lax.ppermute(
            piece, axis, [(i, (i + step) % length) for i in range(length)]
        )
    return total


def head_attention(query, key, value):
    length = query.shape[0]
    score_scale = 1.0 / math.sqrt(query.shape[1])
    query_blocks = query.reshape(length // QUERY_BLOCK, QUERY_BLOCK, query.shape[1])

    def one_block(query_part):
        scores = jnp.dot(query_part, key.T, preferred_element_type=jnp.float32) * score_scale
        expo = jnp.exp(scores - jnp.max(scores, axis=-1, keepdims=True))
        totals = jnp.sum(expo, axis=-1, keepdims=True)
        mixed = jnp.dot(expo.astype(jnp.bfloat16), value, preferred_element_type=jnp.float32)
        return (mixed / totals).astype(jnp.bfloat16)

    return lax.map(one_block, query_blocks).reshape(length, query.shape[1])


def window_columns(volume):
    frame_count = volume.shape[0] - 2
    row_count = volume.shape[1] - 2
    col_count = volume.shape[2] - 2
    pieces = [
        volume[a : a + frame_count, b : b + row_count, c : c + col_count]
        for a in range(3)
        for b in range(3)
        for c in range(3)
    ]
    return jnp.concatenate(pieces, axis=-1).reshape(
        frame_count * row_count * col_count, 27 * volume.shape[3]
    )


def local(
    queries,
    keys_in,
    values_in,
    latent_proj,
    conv_weight,
    conv_bias,
    pool_weight,
    tile_block,
    owner_slot,
):
    group_count = lax.axis_size("seq")
    my_index = lax.axis_index("seq")
    seq_len = S_DEV * group_count
    heads_dev = H // group_count
    quarter = S_DEV // 4

    def to_groups(matrix):
        return matrix.reshape(S_DEV, group_count, heads_dev, HD)

    q_groups, k_groups, v_groups = to_groups(queries), to_groups(keys_in), to_groups(values_in)
    partial = None
    for slot in range(heads_dev):
        stacked = jnp.stack(
            [q_groups[:, :, slot], k_groups[:, :, slot], v_groups[:, :, slot]], axis=2
        )
        gathered = lax.all_to_all(stacked, "seq", split_axis=1, concat_axis=0, tiled=True)
        head_out = head_attention(gathered[:, 0, 0], gathered[:, 0, 1], gathered[:, 0, 2])
        proj_rows = lax.dynamic_slice_in_dim(latent_proj, (my_index * heads_dev + slot) * HD, HD, 0)
        term = jnp.dot(head_out, proj_rows, preferred_element_type=jnp.float32)
        partial = term if partial is None else partial + term

    positions, offsets = halo_tables(group_count)
    token_ids = tile_block[positions] * quarter + offsets
    outgoing = partial[token_ids.reshape(-1)].reshape(group_count, -1, 4 * LC)
    returned = lax.all_to_all(outgoing, "seq", split_axis=0, concat_axis=0, tiled=True)
    tokens = jnp.sum(returned, axis=0).astype(jnp.bfloat16)
    band_row = my_index % TR
    upper_band = band_row == 0
    has_earlier = my_index >= TR

    def to_tile(flat):
        return (
            flat.reshape(FT, RT, WT, 2, 2, LC).transpose(0, 1, 3, 2, 4, 5).reshape(FT, RL, COLS * LC)
        )

    def to_row(flat):
        rows = flat.reshape(FT, WT, 2, 2 * LC)
        return jnp.where(upper_band, rows[:, :, 0], rows[:, :, 1]).reshape(FT, 1, COLS * LC)

    earlier = jnp.where(has_earlier, to_tile(tokens[:S_DEV]), jnp.zeros((), jnp.bfloat16))
    tile_latent = to_tile(tokens[S_DEV : 2 * S_DEV])
    halo_len = FT * WT
    diagonal = jnp.where(
        has_earlier, to_row(tokens[2 * S_DEV : 2 * S_DEV + halo_len]), jnp.zeros((), jnp.bfloat16)
    )
    beside = to_row(tokens[2 * S_DEV + halo_len :])
    extended = jnp.concatenate([earlier, tile_latent], axis=0)
    incoming = jnp.concatenate([diagonal, beside], axis=0)
    above = jnp.where(upper_band, jnp.zeros_like(incoming), incoming)
    below = jnp.where(upper_band, incoming, jnp.zeros_like(incoming))
    volume = jnp.concatenate([above, extended, below], axis=1).reshape(FT + 2, RL + 2, COLS, LC)
    volume = jnp.pad(volume, ((0, 0), (0, 0), (1, 1), (0, 0)))
    kernel = conv_weight.reshape(3, 3, 3, LC, CO)
    pre_act = lax.conv_general_dilated(
        volume[None],
        kernel,
        window_strides=(1, 1, 1),
        padding="VALID",
        dimension_numbers=("NDHWC", "DHWIO", "NDHWC"),
        preferred_element_type=jnp.float32,
    )[0] + conv_bias
    decoded = pre_act.astype(jnp.bfloat16).reshape(1, FT, RL, COLS, CO)
    block_count = BPD * group_count
    band_voxels = group_count // TR * FT * TR * RL * (COLS // block_count)
    weighted = jax.nn.silu(pre_act).reshape(FT, RL, COLS, CO) * pool_weight[0][..., None]
    pooled_term = jnp.sum(weighted, axis=(0, 1)).reshape(block_count, COLS // block_count, CO).sum(
        axis=1
    ) / math.sqrt(band_voxels)
    slots = jnp.arange(block_count, dtype=jnp.int32)
    chooser = (owner_slot[None, :] == slots[:, None]).astype(jnp.float32)
    by_owner = jnp.dot(
        chooser, pooled_term, precision=lax.Precision.HIGHEST, preferred_element_type=jnp.float32
    )
    policy = jnp.sum(
        lax.all_to_all(
            by_owner.reshape(group_count, BPD, CO), "seq", split_axis=0, concat_axis=0, tiled=True
        ),
        axis=0,
    )
    return (decoded, policy)


def solution(mesh):
    placed = (
        P(("roll", "seq"), None),
        P(("roll", "seq"), None),
        P(("roll", "seq"), None),
        P(),
        P(),
        P(),
        P("seq", None, None, None),
        P("roll"),
        P("roll"),
    )
    return jax.shard_map(
        local,
        mesh=mesh,
        in_specs=placed,
        out_specs=(P(("roll", "seq"), None, None, None, None), P(("roll", "seq"), None)),
        check_vma=False,
    )
```

```python
import math

import jax
import numpy as np
import jax.numpy as jnp
from jax import lax
from jax.sharding import PartitionSpec as P

H = 24
HD = 128
LC = 16
CO = 512
S_DEV = 256
RT = 4
WT = 32
TR = 2
BPD = 2
FT = 2
RL = 8
COLS = 64
QUERY_BLOCK = 512


def shifted(array, axis, by):
    length = lax.axis_size(axis)
    pairs = [(i, i + by) for i in range(length) if 0 <= i + by < length]
    return lax.ppermute(array, axis, pairs)


def swapped(array, axis, bit):
    return lax.ppermute(array, axis, [(i, i ^ 1 << bit) for i in range(lax.axis_size(axis))])


def butterfly_sum(array, axis):
    length = lax.axis_size(axis)
    bit = 0
    while (1 << bit) < length:
        array = array + swapped(array, axis, bit)
        bit += 1
    return array


def halo_tokens(tiled, tile):
    token_row = 0 if tile % TR == 0 else RT - 1

    def row_of(source):
        return jnp.concatenate(
            [
                tiled[source, f * RT * WT + token_row * WT : f * RT * WT + (token_row + 1) * WT]
                for f in range(FT)
            ],
            axis=0,
        )

    earlier = tile - TR if tile >= TR else 0
    diagonal = (tile - TR) ^ 1 if tile >= TR else 0
    return jnp.concatenate(
        [tiled[earlier], tiled[tile], row_of(diagonal), row_of(tile ^ 1)], axis=0
    )


def exchange_sum(blocks, axis, my_index):
    length = lax.axis_size(axis)
    total = lax.dynamic_index_in_dim(blocks, my_index, 0, keepdims=False)
    for step in range(1, length):
        piece = lax.dynamic_index_in_dim(blocks, (my_index + step) % length, 0, keepdims=False)
        total = total + lax.ppermute(
            piece, axis, [(i, (i + step) % length) for i in range(length)]
        )
    return total


def head_attention(query, key, value):
    length = query.shape[0]
    score_scale = 1.0 / math.sqrt(query.shape[1])
    query_blocks = query.reshape(length // QUERY_BLOCK, QUERY_BLOCK, query.shape[1])

    def one_block(query_part):
        scores = jnp.dot(query_part, key.T, preferred_element_type=jnp.float32) * score_scale
        expo = jnp.exp(scores - jnp.max(scores, axis=-1, keepdims=True))
        totals = jnp.sum(expo, axis=-1, keepdims=True)
        mixed = jnp.dot(expo.astype(jnp.bfloat16), value, preferred_element_type=jnp.float32)
        return (mixed / totals).astype(jnp.bfloat16)

    return lax.map(one_block, query_blocks).reshape(length, query.shape[1])


def window_columns(volume):
    frame_count = volume.shape[0] - 2
    row_count = volume.shape[1] - 2
    col_count = volume.shape[2] - 2
    pieces = [
        volume[a : a + frame_count, b : b + row_count, c : c + col_count]
        for a in range(3)
        for b in range(3)
        for c in range(3)
    ]
    return jnp.concatenate(pieces, axis=-1).reshape(
        frame_count * row_count * col_count, 27 * volume.shape[3]
    )


def local(
    queries,
    keys_in,
    values_in,
    latent_proj,
    conv_weight,
    conv_bias,
    pool_weight,
    tile_block,
    owner_slot,
):
    group_count = lax.axis_size("seq")
    my_index = lax.axis_index("seq")
    seq_len = S_DEV * group_count
    heads_dev = H // group_count
    quarter = S_DEV // 4

    def to_groups(matrix):
        return matrix.reshape(S_DEV, group_count, heads_dev, HD)

    q_groups, k_groups, v_groups = to_groups(queries), to_groups(keys_in), to_groups(values_in)
    partial = None
    for slot in range(heads_dev):
        stacked = jnp.stack(
            [q_groups[:, :, slot], k_groups[:, :, slot], v_groups[:, :, slot]], axis=0
        )
        gathered = lax.all_to_all(stacked, "seq", split_axis=2, concat_axis=1, tiled=True)
        head_out = head_attention(gathered[0, :, 0], gathered[1, :, 0], gathered[2, :, 0])
        proj_rows = lax.dynamic_slice_in_dim(latent_proj, (my_index * heads_dev + slot) * HD, HD, 0)
        term = jnp.dot(head_out, proj_rows, preferred_element_type=jnp.float32)
        partial = term if partial is None else partial + term

    tiled = partial.reshape(4 * group_count, quarter, 4 * LC)[tile_block]
    tiled = tiled.reshape(group_count, S_DEV, 4 * LC)
    outgoing = jnp.stack([halo_tokens(tiled, tile) for tile in range(group_count)])
    returned = lax.all_to_all(outgoing, "seq", split_axis=0, concat_axis=0, tiled=True)
    tokens = jnp.sum(returned, axis=0).astype(jnp.bfloat16)
    band_row = my_index % TR
    upper_band = band_row == 0
    has_earlier = my_index >= TR

    def to_tile(flat):
        return (
            flat.reshape(FT, RT, WT, 2, 2, LC).transpose(0, 1, 3, 2, 4, 5).reshape(FT, RL, COLS * LC)
        )

    def to_row(flat):
        rows = flat.reshape(FT, WT, 2, 2 * LC)
        return jnp.where(upper_band, rows[:, :, 0], rows[:, :, 1]).reshape(FT, 1, COLS * LC)

    earlier = jnp.where(has_earlier, to_tile(tokens[:S_DEV]), jnp.zeros((), jnp.bfloat16))
    tile_latent = to_tile(tokens[S_DEV : 2 * S_DEV])
    halo_len = FT * WT
    diagonal = jnp.where(
        has_earlier, to_row(tokens[2 * S_DEV : 2 * S_DEV + halo_len]), jnp.zeros((), jnp.bfloat16)
    )
    beside = to_row(tokens[2 * S_DEV + halo_len :])
    extended = jnp.concatenate([earlier, tile_latent], axis=0)
    incoming = jnp.concatenate([diagonal, beside], axis=0)
    above = jnp.where(upper_band, jnp.zeros_like(incoming), incoming)
    below = jnp.where(upper_band, incoming, jnp.zeros_like(incoming))
    volume = jnp.concatenate([above, extended, below], axis=1).reshape(FT + 2, RL + 2, COLS, LC)
    volume = jnp.pad(volume, ((0, 0), (0, 0), (1, 1), (0, 0)))
    kernel = conv_weight.reshape(3, 3, 3, LC, CO)
    pre_act = lax.conv_general_dilated(
        volume[None],
        kernel,
        window_strides=(1, 1, 1),
        padding="VALID",
        dimension_numbers=("NDHWC", "DHWIO", "NDHWC"),
        preferred_element_type=jnp.float32,
    )[0] + conv_bias
    decoded = pre_act.astype(jnp.bfloat16).reshape(1, FT, RL, COLS, CO)
    block_count = BPD * group_count
    band_voxels = group_count // TR * FT * TR * RL * (COLS // block_count)
    weighted = jax.nn.silu(pre_act).reshape(FT, RL, COLS, CO) * pool_weight[0][..., None]
    pooled_term = jnp.sum(weighted, axis=(0, 1)).reshape(block_count, COLS // block_count, CO).sum(
        axis=1
    ) / math.sqrt(band_voxels)
    slots = jnp.arange(block_count, dtype=jnp.int32)
    chooser = (owner_slot[None, :] == slots[:, None]).astype(jnp.float32)
    by_owner = jnp.dot(
        chooser, pooled_term, precision=lax.Precision.HIGHEST, preferred_element_type=jnp.float32
    )
    policy = jnp.sum(
        lax.all_to_all(
            by_owner.reshape(group_count, BPD, CO), "seq", split_axis=0, concat_axis=0, tiled=True
        ),
        axis=0,
    )
    return (decoded, policy)


def solution(mesh):
    placed = (
        P(("roll", "seq"), None),
        P(("roll", "seq"), None),
        P(("roll", "seq"), None),
        P(),
        P(),
        P(),
        P("seq", None, None, None),
        P("roll"),
        P("roll"),
    )
    return jax.shard_map(
        local,
        mesh=mesh,
        in_specs=placed,
        out_specs=(P(("roll", "seq"), None, None, None, None), P(("roll", "seq"), None)),
        check_vma=False,
    )
```

```python
import math

import jax
import numpy as np
import jax.numpy as jnp
from jax import lax
from jax.sharding import PartitionSpec as P

H = 24
HD = 128
LC = 16
CO = 512
S_DEV = 256
RT = 4
WT = 32
TR = 2
BPD = 2
FT = 2
RL = 8
COLS = 64
QUERY_BLOCK = 512


def shifted(array, axis, by):
    length = lax.axis_size(axis)
    pairs = [(i, i + by) for i in range(length) if 0 <= i + by < length]
    return lax.ppermute(array, axis, pairs)


def swapped(array, axis, bit):
    return lax.ppermute(array, axis, [(i, i ^ 1 << bit) for i in range(lax.axis_size(axis))])


def butterfly_sum(array, axis):
    length = lax.axis_size(axis)
    bit = 0
    while (1 << bit) < length:
        array = array + swapped(array, axis, bit)
        bit += 1
    return array


def halo_tables(tile_count):
    positions, halves = [], []
    for tile in range(tile_count):
        lower = 0 if tile % TR == 0 else 1
        earlier = tile - TR if tile >= TR else 0
        diagonal = (tile - TR) ^ 1 if tile >= TR else 0
        pos, half = [], []
        for src in (earlier, tile):
            for q in range(4):
                pos += [4 * src + q, 4 * src + q]
                half += [0, 1]
        for src in (diagonal, tile ^ 1):
            for f in range(FT):
                pos.append(4 * src + 2 * f + lower)
                half.append(lower)
        positions.append(pos)
        halves.append(half)
    return np.array(positions, np.int32), np.array(halves, np.int32)


def exchange_sum(blocks, axis, my_index):
    length = lax.axis_size(axis)
    total = lax.dynamic_index_in_dim(blocks, my_index, 0, keepdims=False)
    for step in range(1, length):
        piece = lax.dynamic_index_in_dim(blocks, (my_index + step) % length, 0, keepdims=False)
        total = total + lax.ppermute(
            piece, axis, [(i, (i + step) % length) for i in range(length)]
        )
    return total


def head_attention(query, key, value):
    length = query.shape[0]
    score_scale = 1.0 / math.sqrt(query.shape[1])
    query_blocks = query.reshape(length // QUERY_BLOCK, QUERY_BLOCK, query.shape[1])

    def one_block(query_part):
        scores = jnp.dot(query_part, key.T, preferred_element_type=jnp.float32) * score_scale
        expo = jnp.exp(scores - jnp.max(scores, axis=-1, keepdims=True))
        totals = jnp.sum(expo, axis=-1, keepdims=True)
        mixed = jnp.dot(expo.astype(jnp.bfloat16), value, preferred_element_type=jnp.float32)
        return (mixed / totals).astype(jnp.bfloat16)

    return lax.map(one_block, query_blocks).reshape(length, query.shape[1])


def window_columns(volume):
    frame_count = volume.shape[0] - 2
    row_count = volume.shape[1] - 2
    col_count = volume.shape[2] - 2
    pieces = [
        volume[a : a + frame_count, b : b + row_count, c : c + col_count]
        for a in range(3)
        for b in range(3)
        for c in range(3)
    ]
    return jnp.concatenate(pieces, axis=-1).reshape(
        frame_count * row_count * col_count, 27 * volume.shape[3]
    )


def local(
    queries,
    keys_in,
    values_in,
    latent_proj,
    conv_weight,
    conv_bias,
    pool_weight,
    tile_block,
    owner_slot,
):
    group_count = lax.axis_size("seq")
    my_index = lax.axis_index("seq")
    seq_len = S_DEV * group_count
    heads_dev = H // group_count
    quarter = S_DEV // 4

    slot_width = group_count * HD
    partial = None
    for slot in range(heads_dev):
        columns = slice(slot * slot_width, (slot + 1) * slot_width)
        stacked = jnp.stack(
            [queries[:, columns], keys_in[:, columns], values_in[:, columns]], axis=0
        ).reshape(3, S_DEV, group_count, HD)
        gathered = lax.all_to_all(stacked, "seq", split_axis=2, concat_axis=1, tiled=True)
        head_out = head_attention(gathered[0, :, 0], gathered[1, :, 0], gathered[2, :, 0])
        proj_rows = lax.dynamic_slice_in_dim(latent_proj, (slot * group_count + my_index) * HD, HD, 0)
        term = jnp.dot(head_out, proj_rows, preferred_element_type=jnp.float32)
        partial = term if partial is None else partial + term

    positions, halves = halo_tables(group_count)
    picks = jnp.sum(
        jnp.where(positions[..., None] == np.arange(4 * group_count), tile_block, 0), axis=-1
    )
    half_pieces = partial.reshape(8 * group_count, quarter // 2, 4 * LC)
    outgoing = half_pieces[picks * 2 + halves].reshape(group_count, -1, 4 * LC)
    returned = lax.all_to_all(outgoing, "seq", split_axis=0, concat_axis=0, tiled=True)
    tokens = jnp.sum(returned, axis=0).astype(jnp.bfloat16)
    band_row = my_index % TR
    upper_band = band_row == 0
    has_earlier = my_index >= TR

    def to_tile(flat):
        return (
            flat.reshape(FT, RT, WT, 2, 2, LC).transpose(0, 1, 3, 2, 4, 5).reshape(FT, RL, COLS * LC)
        )

    def to_row(flat):
        rows = flat.reshape(FT, WT, 2, 2 * LC)
        return jnp.where(upper_band, rows[:, :, 0], rows[:, :, 1]).reshape(FT, 1, COLS * LC)

    earlier = jnp.where(has_earlier, to_tile(tokens[:S_DEV]), jnp.zeros((), jnp.bfloat16))
    tile_latent = to_tile(tokens[S_DEV : 2 * S_DEV])
    halo_len = FT * WT
    diagonal = jnp.where(
        has_earlier, to_row(tokens[2 * S_DEV : 2 * S_DEV + halo_len]), jnp.zeros((), jnp.bfloat16)
    )
    beside = to_row(tokens[2 * S_DEV + halo_len :])
    extended = jnp.concatenate([earlier, tile_latent], axis=0)
    incoming = jnp.concatenate([diagonal, beside], axis=0)
    above = jnp.where(upper_band, jnp.zeros_like(incoming), incoming)
    below = jnp.where(upper_band, incoming, jnp.zeros_like(incoming))
    volume = jnp.concatenate([above, extended, below], axis=1).reshape(FT + 2, RL + 2, COLS, LC)
    volume = jnp.pad(volume, ((0, 0), (0, 0), (1, 1), (0, 0)))
    kernel = conv_weight.reshape(3, 3, 3, LC, CO)
    pre_act = lax.conv_general_dilated(
        volume[None],
        kernel,
        window_strides=(1, 1, 1),
        padding="VALID",
        dimension_numbers=("NDHWC", "DHWIO", "NDHWC"),
        preferred_element_type=jnp.float32,
    )[0] + conv_bias
    decoded = pre_act.astype(jnp.bfloat16).reshape(1, FT, RL, COLS, CO)
    block_count = BPD * group_count
    band_voxels = group_count // TR * FT * TR * RL * (COLS // block_count)
    weighted = jax.nn.silu(pre_act).reshape(FT, RL, COLS, CO) * pool_weight[0][..., None]
    pooled_term = jnp.sum(weighted, axis=(0, 1)).reshape(block_count, COLS // block_count, CO).sum(
        axis=1
    ) / math.sqrt(band_voxels)
    slots = jnp.arange(block_count, dtype=jnp.int32)
    chooser = (owner_slot[None, :] == slots[:, None]).astype(jnp.float32)
    by_owner = jnp.dot(
        chooser, pooled_term, precision=lax.Precision.HIGHEST, preferred_element_type=jnp.float32
    )
    policy = jnp.sum(
        lax.all_to_all(
            by_owner.reshape(group_count, BPD, CO), "seq", split_axis=0, concat_axis=0, tiled=True
        ),
        axis=0,
    )
    return (decoded, policy)


def solution(mesh):
    placed = (
        P(("roll", "seq"), None),
        P(("roll", "seq"), None),
        P(("roll", "seq"), None),
        P(),
        P(),
        P(),
        P("seq", None, None, None),
        P("roll"),
        P("roll"),
    )
    return jax.shard_map(
        local,
        mesh=mesh,
        in_specs=placed,
        out_specs=(P(("roll", "seq"), None, None, None, None), P(("roll", "seq"), None)),
        check_vma=False,
    )
```

```python
import math

import jax
import numpy as np
import jax.numpy as jnp
from jax import lax
from jax.experimental import pallas as pl
from jax.experimental.pallas import tpu as pltpu
from jax.sharding import PartitionSpec as P

H = 24
HD = 128
LC = 16
CO = 512
S_DEV = 256
RT = 4
WT = 32
TR = 2
BPD = 2
FT = 2
RL = 8
COLS = 64
QUERY_BLOCK = 512


def shifted(array, axis, by):
    length = lax.axis_size(axis)
    pairs = [(i, i + by) for i in range(length) if 0 <= i + by < length]
    return lax.ppermute(array, axis, pairs)


def swapped(array, axis, bit):
    return lax.ppermute(array, axis, [(i, i ^ 1 << bit) for i in range(lax.axis_size(axis))])


def butterfly_sum(array, axis):
    length = lax.axis_size(axis)
    bit = 0
    while (1 << bit) < length:
        array = array + swapped(array, axis, bit)
        bit += 1
    return array


def halo_tables(tile_count):
    positions, halves = [], []
    for tile in range(tile_count):
        lower = 0 if tile % TR == 0 else 1
        earlier = tile - TR if tile >= TR else 0
        diagonal = (tile - TR) ^ 1 if tile >= TR else 0
        pos, half = [], []
        for src in (earlier, tile):
            for q in range(4):
                pos += [4 * src + q, 4 * src + q]
                half += [0, 1]
        for src in (diagonal, tile ^ 1):
            for f in range(FT):
                pos.append(4 * src + 2 * f + lower)
                half.append(lower)
        positions.append(pos)
        halves.append(half)
    return np.array(positions, np.int32), np.array(halves, np.int32)


def exchange_sum(blocks, axis, my_index):
    length = lax.axis_size(axis)
    total = lax.dynamic_index_in_dim(blocks, my_index, 0, keepdims=False)
    for step in range(1, length):
        piece = lax.dynamic_index_in_dim(blocks, (my_index + step) % length, 0, keepdims=False)
        total = total + lax.ppermute(
            piece, axis, [(i, (i + step) % length) for i in range(length)]
        )
    return total


def slot_operand(queries, keys_in, values_in, slot, group_count):
    sources = (queries, keys_in, values_in)
    base = slot * group_count * HD

    def kernel(q_ref, k_ref, v_ref, out_ref, sems):
        copies = []
        for part, src in enumerate((q_ref, k_ref, v_ref)):
            for group in range(group_count):
                copy = pltpu.make_async_copy(
                    src.at[:, pl.ds(base + group * HD, HD)],
                    out_ref.at[group, part],
                    sems.at[part * group_count + group],
                )
                copy.start()
                copies.append(copy)
        for copy in copies:
            copy.wait()

    return pl.pallas_call(
        kernel,
        out_shape=jax.ShapeDtypeStruct((group_count, 3, S_DEV, HD), queries.dtype),
        in_specs=[pl.BlockSpec(memory_space=pl.ANY)] * 3,
        out_specs=pl.BlockSpec(memory_space=pl.ANY),
        scratch_shapes=[pltpu.SemaphoreType.DMA((3 * group_count,))],
    )(*sources)


def head_attention(query, key, value):
    length = query.shape[0]
    score_scale = 1.0 / math.sqrt(query.shape[1])
    query_blocks = query.reshape(length // QUERY_BLOCK, QUERY_BLOCK, query.shape[1])

    def one_block(query_part):
        scores = jnp.dot(query_part, key.T, preferred_element_type=jnp.float32) * score_scale
        expo = jnp.exp(scores - jnp.max(scores, axis=-1, keepdims=True))
        totals = jnp.sum(expo, axis=-1, keepdims=True)
        mixed = jnp.dot(expo.astype(jnp.bfloat16), value, preferred_element_type=jnp.float32)
        return (mixed / totals).astype(jnp.bfloat16)

    return lax.map(one_block, query_blocks).reshape(length, query.shape[1])


def window_columns(volume):
    frame_count = volume.shape[0] - 2
    row_count = volume.shape[1] - 2
    col_count = volume.shape[2] - 2
    pieces = [
        volume[a : a + frame_count, b : b + row_count, c : c + col_count]
        for a in range(3)
        for b in range(3)
        for c in range(3)
    ]
    return jnp.concatenate(pieces, axis=-1).reshape(
        frame_count * row_count * col_count, 27 * volume.shape[3]
    )


def local(
    queries,
    keys_in,
    values_in,
    latent_proj,
    conv_weight,
    conv_bias,
    pool_weight,
    tile_block,
    owner_slot,
):
    group_count = lax.axis_size("seq")
    my_index = lax.axis_index("seq")
    seq_len = S_DEV * group_count
    heads_dev = H // group_count
    quarter = S_DEV // 4

    partial = None
    for slot in range(heads_dev):
        stacked = slot_operand(queries, keys_in, values_in, slot, group_count)
        gathered = lax.all_to_all(stacked, "seq", split_axis=0, concat_axis=0, tiled=True)
        head_out = head_attention(
            *(gathered[:, part].reshape(seq_len, HD) for part in range(3))
        )
        proj_rows = lax.dynamic_slice_in_dim(latent_proj, (slot * group_count + my_index) * HD, HD, 0)
        term = jnp.dot(head_out, proj_rows, preferred_element_type=jnp.float32)
        partial = term if partial is None else partial + term

    positions, halves = halo_tables(group_count)
    picks = jnp.sum(
        jnp.where(positions[..., None] == np.arange(4 * group_count), tile_block, 0), axis=-1
    )
    half_pieces = partial.reshape(8 * group_count, quarter // 2, 4 * LC)
    outgoing = half_pieces[picks * 2 + halves].reshape(group_count, -1, 4 * LC)
    returned = lax.all_to_all(outgoing, "seq", split_axis=0, concat_axis=0, tiled=True)
    tokens = jnp.sum(returned, axis=0).astype(jnp.bfloat16)
    band_row = my_index % TR
    upper_band = band_row == 0
    has_earlier = my_index >= TR

    def to_tile(flat):
        return (
            flat.reshape(FT, RT, WT, 2, 2, LC).transpose(0, 1, 3, 2, 4, 5).reshape(FT, RL, COLS * LC)
        )

    def to_row(flat):
        rows = flat.reshape(FT, WT, 2, 2 * LC)
        return jnp.where(upper_band, rows[:, :, 0], rows[:, :, 1]).reshape(FT, 1, COLS * LC)

    earlier = jnp.where(has_earlier, to_tile(tokens[:S_DEV]), jnp.zeros((), jnp.bfloat16))
    tile_latent = to_tile(tokens[S_DEV : 2 * S_DEV])
    halo_len = FT * WT
    diagonal = jnp.where(
        has_earlier, to_row(tokens[2 * S_DEV : 2 * S_DEV + halo_len]), jnp.zeros((), jnp.bfloat16)
    )
    beside = to_row(tokens[2 * S_DEV + halo_len :])
    extended = jnp.concatenate([earlier, tile_latent], axis=0)
    incoming = jnp.concatenate([diagonal, beside], axis=0)
    above = jnp.where(upper_band, jnp.zeros_like(incoming), incoming)
    below = jnp.where(upper_band, incoming, jnp.zeros_like(incoming))
    volume = jnp.concatenate([above, extended, below], axis=1).reshape(FT + 2, RL + 2, COLS, LC)
    volume = jnp.pad(volume, ((0, 0), (0, 0), (1, 1), (0, 0)))
    kernel = conv_weight.reshape(3, 3, 3, LC, CO)
    pre_act = lax.conv_general_dilated(
        volume[None],
        kernel,
        window_strides=(1, 1, 1),
        padding="VALID",
        dimension_numbers=("NDHWC", "DHWIO", "NDHWC"),
        preferred_element_type=jnp.float32,
    )[0] + conv_bias
    decoded = pre_act.astype(jnp.bfloat16).reshape(1, FT, RL, COLS, CO)
    block_count = BPD * group_count
    band_voxels = group_count // TR * FT * TR * RL * (COLS // block_count)
    weighted = jax.nn.silu(pre_act).reshape(FT, RL, COLS, CO) * pool_weight[0][..., None]
    pooled_term = jnp.sum(weighted, axis=(0, 1)).reshape(block_count, COLS // block_count, CO).sum(
        axis=1
    ) / math.sqrt(band_voxels)
    slots = jnp.arange(block_count, dtype=jnp.int32)
    chooser = (owner_slot[None, :] == slots[:, None]).astype(jnp.float32)
    by_owner = jnp.dot(
        chooser, pooled_term, precision=lax.Precision.HIGHEST, preferred_element_type=jnp.float32
    )
    policy = jnp.sum(
        lax.all_to_all(
            by_owner.reshape(group_count, BPD, CO), "seq", split_axis=0, concat_axis=0, tiled=True
        ),
        axis=0,
    )
    return (decoded, policy)


def solution(mesh):
    placed = (
        P(("roll", "seq"), None),
        P(("roll", "seq"), None),
        P(("roll", "seq"), None),
        P(),
        P(),
        P(),
        P("seq", None, None, None),
        P("roll"),
        P("roll"),
    )
    return jax.shard_map(
        local,
        mesh=mesh,
        in_specs=placed,
        out_specs=(P(("roll", "seq"), None, None, None, None), P(("roll", "seq"), None)),
        check_vma=False,
    )
```

```python
import math

import jax
import numpy as np
import jax.numpy as jnp
from jax import lax
from jax.experimental import pallas as pl
from jax.experimental.pallas import tpu as pltpu
from jax.sharding import PartitionSpec as P

H = 24
HD = 128
LC = 16
CO = 512
S_DEV = 256
RT = 4
WT = 32
TR = 2
BPD = 2
FT = 2
RL = 8
COLS = 64
QUERY_BLOCK = 512


def shifted(array, axis, by):
    length = lax.axis_size(axis)
    pairs = [(i, i + by) for i in range(length) if 0 <= i + by < length]
    return lax.ppermute(array, axis, pairs)


def swapped(array, axis, bit):
    return lax.ppermute(array, axis, [(i, i ^ 1 << bit) for i in range(lax.axis_size(axis))])


def butterfly_sum(array, axis):
    length = lax.axis_size(axis)
    bit = 0
    while (1 << bit) < length:
        array = array + swapped(array, axis, bit)
        bit += 1
    return array


def halo_tables(tile_count):
    positions, halves = [], []
    for tile in range(tile_count):
        lower = 0 if tile % TR == 0 else 1
        earlier = tile - TR if tile >= TR else 0
        diagonal = (tile - TR) ^ 1 if tile >= TR else 0
        pos, half = [], []
        for src in (earlier, tile):
            for q in range(4):
                pos += [4 * src + q, 4 * src + q]
                half += [0, 1]
        for src in (diagonal, tile ^ 1):
            for f in range(FT):
                pos.append(4 * src + 2 * f + lower)
                half.append(lower)
        positions.append(pos)
        halves.append(half)
    return np.array(positions, np.int32), np.array(halves, np.int32)


def exchange_sum(blocks, axis, my_index):
    length = lax.axis_size(axis)
    total = lax.dynamic_index_in_dim(blocks, my_index, 0, keepdims=False)
    for step in range(1, length):
        piece = lax.dynamic_index_in_dim(blocks, (my_index + step) % length, 0, keepdims=False)
        total = total + lax.ppermute(
            piece, axis, [(i, (i + step) % length) for i in range(length)]
        )
    return total


def slot_operand(queries, keys_in, values_in, slot, group_count):
    width = group_count * HD

    def kernel(q_ref, k_ref, v_ref, out_ref):
        for part, src in enumerate((q_ref, k_ref, v_ref)):
            for group in range(group_count):
                out_ref[group, part] = src[:, group * HD : (group + 1) * HD]

    block = pl.BlockSpec((S_DEV, width), lambda i: (0, slot))
    return pl.pallas_call(
        kernel,
        grid=(1,),
        out_shape=jax.ShapeDtypeStruct((group_count, 3, S_DEV, HD), queries.dtype),
        in_specs=[block] * 3,
        out_specs=pl.BlockSpec((group_count, 3, S_DEV, HD), lambda i: (0, 0, 0, 0)),
    )(queries, keys_in, values_in)


def head_attention(query, key, value):
    length = query.shape[0]
    score_scale = 1.0 / math.sqrt(query.shape[1])
    query_blocks = query.reshape(length // QUERY_BLOCK, QUERY_BLOCK, query.shape[1])

    def one_block(query_part):
        scores = jnp.dot(query_part, key.T, preferred_element_type=jnp.float32) * score_scale
        expo = jnp.exp(scores - jnp.max(scores, axis=-1, keepdims=True))
        totals = jnp.sum(expo, axis=-1, keepdims=True)
        mixed = jnp.dot(expo.astype(jnp.bfloat16), value, preferred_element_type=jnp.float32)
        return (mixed / totals).astype(jnp.bfloat16)

    return lax.map(one_block, query_blocks).reshape(length, query.shape[1])


def window_columns(volume):
    frame_count = volume.shape[0] - 2
    row_count = volume.shape[1] - 2
    col_count = volume.shape[2] - 2
    pieces = [
        volume[a : a + frame_count, b : b + row_count, c : c + col_count]
        for a in range(3)
        for b in range(3)
        for c in range(3)
    ]
    return jnp.concatenate(pieces, axis=-1).reshape(
        frame_count * row_count * col_count, 27 * volume.shape[3]
    )


def local(
    queries,
    keys_in,
    values_in,
    latent_proj,
    conv_weight,
    conv_bias,
    pool_weight,
    tile_block,
    owner_slot,
):
    group_count = lax.axis_size("seq")
    my_index = lax.axis_index("seq")
    seq_len = S_DEV * group_count
    heads_dev = H // group_count
    quarter = S_DEV // 4

    partial = None
    for slot in range(heads_dev):
        stacked = slot_operand(queries, keys_in, values_in, slot, group_count)
        gathered = lax.all_to_all(stacked, "seq", split_axis=0, concat_axis=0, tiled=True)
        head_out = head_attention(
            *(gathered[:, part].reshape(seq_len, HD) for part in range(3))
        )
        proj_rows = lax.dynamic_slice_in_dim(latent_proj, (slot * group_count + my_index) * HD, HD, 0)
        term = jnp.dot(head_out, proj_rows, preferred_element_type=jnp.float32)
        partial = term if partial is None else partial + term

    positions, halves = halo_tables(group_count)
    picks = jnp.sum(
        jnp.where(positions[..., None] == np.arange(4 * group_count), tile_block, 0), axis=-1
    )
    half_pieces = partial.reshape(8 * group_count, quarter // 2, 4 * LC)
    outgoing = half_pieces[picks * 2 + halves].reshape(group_count, -1, 4 * LC)
    returned = lax.all_to_all(outgoing, "seq", split_axis=0, concat_axis=0, tiled=True)
    tokens = jnp.sum(returned, axis=0).astype(jnp.bfloat16)
    band_row = my_index % TR
    upper_band = band_row == 0
    has_earlier = my_index >= TR

    def to_tile(flat):
        return (
            flat.reshape(FT, RT, WT, 2, 2, LC).transpose(0, 1, 3, 2, 4, 5).reshape(FT, RL, COLS * LC)
        )

    def to_row(flat):
        rows = flat.reshape(FT, WT, 2, 2 * LC)
        return jnp.where(upper_band, rows[:, :, 0], rows[:, :, 1]).reshape(FT, 1, COLS * LC)

    earlier = jnp.where(has_earlier, to_tile(tokens[:S_DEV]), jnp.zeros((), jnp.bfloat16))
    tile_latent = to_tile(tokens[S_DEV : 2 * S_DEV])
    halo_len = FT * WT
    diagonal = jnp.where(
        has_earlier, to_row(tokens[2 * S_DEV : 2 * S_DEV + halo_len]), jnp.zeros((), jnp.bfloat16)
    )
    beside = to_row(tokens[2 * S_DEV + halo_len :])
    extended = jnp.concatenate([earlier, tile_latent], axis=0)
    incoming = jnp.concatenate([diagonal, beside], axis=0)
    above = jnp.where(upper_band, jnp.zeros_like(incoming), incoming)
    below = jnp.where(upper_band, incoming, jnp.zeros_like(incoming))
    volume = jnp.concatenate([above, extended, below], axis=1).reshape(FT + 2, RL + 2, COLS, LC)
    volume = jnp.pad(volume, ((0, 0), (0, 0), (1, 1), (0, 0)))
    kernel = conv_weight.reshape(3, 3, 3, LC, CO)
    pre_act = lax.conv_general_dilated(
        volume[None],
        kernel,
        window_strides=(1, 1, 1),
        padding="VALID",
        dimension_numbers=("NDHWC", "DHWIO", "NDHWC"),
        preferred_element_type=jnp.float32,
    )[0] + conv_bias
    decoded = pre_act.astype(jnp.bfloat16).reshape(1, FT, RL, COLS, CO)
    block_count = BPD * group_count
    band_voxels = group_count // TR * FT * TR * RL * (COLS // block_count)
    weighted = jax.nn.silu(pre_act).reshape(FT, RL, COLS, CO) * pool_weight[0][..., None]
    pooled_term = jnp.sum(weighted, axis=(0, 1)).reshape(block_count, COLS // block_count, CO).sum(
        axis=1
    ) / math.sqrt(band_voxels)
    slots = jnp.arange(block_count, dtype=jnp.int32)
    chooser = (owner_slot[None, :] == slots[:, None]).astype(jnp.float32)
    by_owner = jnp.dot(
        chooser, pooled_term, precision=lax.Precision.HIGHEST, preferred_element_type=jnp.float32
    )
    policy = jnp.sum(
        lax.all_to_all(
            by_owner.reshape(group_count, BPD, CO), "seq", split_axis=0, concat_axis=0, tiled=True
        ),
        axis=0,
    )
    return (decoded, policy)


def solution(mesh):
    placed = (
        P(("roll", "seq"), None),
        P(("roll", "seq"), None),
        P(("roll", "seq"), None),
        P(),
        P(),
        P(),
        P("seq", None, None, None),
        P("roll"),
        P("roll"),
    )
    return jax.shard_map(
        local,
        mesh=mesh,
        in_specs=placed,
        out_specs=(P(("roll", "seq"), None, None, None, None), P(("roll", "seq"), None)),
        check_vma=False,
    )
```

```python
import math

import jax
import numpy as np
import jax.numpy as jnp
from jax import lax
from jax.experimental import pallas as pl
from jax.experimental.pallas import tpu as pltpu
from jax.sharding import PartitionSpec as P

H = 24
HD = 128
LC = 16
CO = 512
S_DEV = 256
RT = 4
WT = 32
TR = 2
BPD = 2
FT = 2
RL = 8
COLS = 64
QUERY_BLOCK = 512


def shifted(array, axis, by):
    length = lax.axis_size(axis)
    pairs = [(i, i + by) for i in range(length) if 0 <= i + by < length]
    return lax.ppermute(array, axis, pairs)


def swapped(array, axis, bit):
    return lax.ppermute(array, axis, [(i, i ^ 1 << bit) for i in range(lax.axis_size(axis))])


def butterfly_sum(array, axis):
    length = lax.axis_size(axis)
    bit = 0
    while (1 << bit) < length:
        array = array + swapped(array, axis, bit)
        bit += 1
    return array


def halo_tables(tile_count):
    positions, halves = [], []
    for tile in range(tile_count):
        lower = 0 if tile % TR == 0 else 1
        earlier = tile - TR if tile >= TR else 0
        diagonal = (tile - TR) ^ 1 if tile >= TR else 0
        pos, half = [], []
        for src in (earlier, tile):
            for q in range(4):
                pos += [4 * src + q, 4 * src + q]
                half += [0, 1]
        for src in (diagonal, tile ^ 1):
            for f in range(FT):
                pos.append(4 * src + 2 * f + lower)
                half.append(lower)
        positions.append(pos)
        halves.append(half)
    return np.array(positions, np.int32), np.array(halves, np.int32)


def exchange_sum(blocks, axis, my_index):
    length = lax.axis_size(axis)
    total = lax.dynamic_index_in_dim(blocks, my_index, 0, keepdims=False)
    for step in range(1, length):
        piece = lax.dynamic_index_in_dim(blocks, (my_index + step) % length, 0, keepdims=False)
        total = total + lax.ppermute(
            piece, axis, [(i, (i + step) % length) for i in range(length)]
        )
    return total


def slot_operand(queries, keys_in, values_in, slot, group_count):
    width = group_count * HD

    def kernel(q_ref, k_ref, v_ref, out_ref):
        for part, src in enumerate((q_ref, k_ref, v_ref)):
            for group in range(group_count):
                out_ref[group, part] = src[:, group * HD : (group + 1) * HD]

    block = pl.BlockSpec((S_DEV, width), lambda i: (0, slot))
    return pl.pallas_call(
        kernel,
        grid=(1,),
        out_shape=jax.ShapeDtypeStruct((group_count, 3, S_DEV, HD), queries.dtype),
        in_specs=[block] * 3,
        out_specs=pl.BlockSpec((group_count, 3, S_DEV, HD), lambda i: (0, 0, 0, 0)),
    )(queries, keys_in, values_in)


def head_attention(query, key, value, proj_rows):
    length = query.shape[0]
    score_scale = 1.0 / math.sqrt(query.shape[1])
    query_blocks = query.reshape(length // QUERY_BLOCK, QUERY_BLOCK, query.shape[1])

    def one_block(query_part):
        scores = jnp.dot(query_part, key.T, preferred_element_type=jnp.float32) * score_scale
        expo = jnp.exp(scores - jnp.max(scores, axis=-1, keepdims=True))
        totals = jnp.sum(expo, axis=-1, keepdims=True)
        mixed = jnp.dot(expo.astype(jnp.bfloat16), value, preferred_element_type=jnp.float32)
        head_out = (mixed / totals).astype(jnp.bfloat16)
        return jnp.dot(head_out, proj_rows, preferred_element_type=jnp.float32)

    return lax.map(one_block, query_blocks).reshape(length, proj_rows.shape[1])


def window_columns(volume):
    frame_count = volume.shape[0] - 2
    row_count = volume.shape[1] - 2
    col_count = volume.shape[2] - 2
    pieces = [
        volume[a : a + frame_count, b : b + row_count, c : c + col_count]
        for a in range(3)
        for b in range(3)
        for c in range(3)
    ]
    return jnp.concatenate(pieces, axis=-1).reshape(
        frame_count * row_count * col_count, 27 * volume.shape[3]
    )


def local(
    queries,
    keys_in,
    values_in,
    latent_proj,
    conv_weight,
    conv_bias,
    pool_weight,
    tile_block,
    owner_slot,
):
    group_count = lax.axis_size("seq")
    my_index = lax.axis_index("seq")
    seq_len = S_DEV * group_count
    heads_dev = H // group_count
    quarter = S_DEV // 4

    partial = None
    for slot in range(heads_dev):
        stacked = slot_operand(queries, keys_in, values_in, slot, group_count)
        gathered = lax.all_to_all(stacked, "seq", split_axis=0, concat_axis=0, tiled=True)
        proj_rows = lax.dynamic_slice_in_dim(latent_proj, (slot * group_count + my_index) * HD, HD, 0)
        term = head_attention(
            *(gathered[:, part].reshape(seq_len, HD) for part in range(3)), proj_rows
        )
        partial = term if partial is None else partial + term

    positions, halves = halo_tables(group_count)
    picks = jnp.sum(
        jnp.where(positions[..., None] == np.arange(4 * group_count), tile_block, 0), axis=-1
    )
    half_pieces = partial.reshape(8 * group_count, quarter // 4, 8 * LC)
    outgoing = half_pieces[picks * 2 + halves].reshape(group_count, -1, 8 * LC)
    returned = lax.all_to_all(outgoing, "seq", split_axis=0, concat_axis=0, tiled=True)
    tokens = jnp.sum(returned, axis=0).reshape(-1, 4 * LC).astype(jnp.bfloat16)
    band_row = my_index % TR
    upper_band = band_row == 0
    has_earlier = my_index >= TR

    def to_tile(flat):
        return (
            flat.reshape(FT, RT, WT, 2, 2, LC).transpose(0, 1, 3, 2, 4, 5).reshape(FT, RL, COLS * LC)
        )

    def to_row(flat):
        rows = flat.reshape(FT, WT, 2, 2 * LC)
        return jnp.where(upper_band, rows[:, :, 0], rows[:, :, 1]).reshape(FT, 1, COLS * LC)

    earlier = jnp.where(has_earlier, to_tile(tokens[:S_DEV]), jnp.zeros((), jnp.bfloat16))
    tile_latent = to_tile(tokens[S_DEV : 2 * S_DEV])
    halo_len = FT * WT
    diagonal = jnp.where(
        has_earlier, to_row(tokens[2 * S_DEV : 2 * S_DEV + halo_len]), jnp.zeros((), jnp.bfloat16)
    )
    beside = to_row(tokens[2 * S_DEV + halo_len :])
    extended = jnp.concatenate([earlier, tile_latent], axis=0)
    incoming = jnp.concatenate([diagonal, beside], axis=0)
    above = jnp.where(upper_band, jnp.zeros_like(incoming), incoming)
    below = jnp.where(upper_band, incoming, jnp.zeros_like(incoming))
    volume = jnp.concatenate([above, extended, below], axis=1).reshape(FT + 2, RL + 2, COLS, LC)
    volume = jnp.pad(volume, ((0, 0), (0, 0), (1, 1), (0, 0)))
    kernel = conv_weight.reshape(3, 3, 3, LC, CO)
    pre_act = lax.conv_general_dilated(
        volume[None],
        kernel,
        window_strides=(1, 1, 1),
        padding="VALID",
        dimension_numbers=("NDHWC", "DHWIO", "NDHWC"),
        preferred_element_type=jnp.float32,
    )[0] + conv_bias
    decoded = pre_act.astype(jnp.bfloat16).reshape(1, FT, RL, COLS, CO)
    block_count = BPD * group_count
    band_voxels = group_count // TR * FT * TR * RL * (COLS // block_count)
    weighted = jax.nn.silu(pre_act).reshape(FT, RL, COLS, CO) * pool_weight[0][..., None]
    pooled_term = jnp.sum(weighted, axis=(0, 1)).reshape(block_count, COLS // block_count, CO).sum(
        axis=1
    ) / math.sqrt(band_voxels)
    slots = jnp.arange(block_count, dtype=jnp.int32)
    chooser = (owner_slot[None, :] == slots[:, None]).astype(jnp.float32)
    by_owner = jnp.dot(
        chooser, pooled_term, precision=lax.Precision.HIGHEST, preferred_element_type=jnp.float32
    )
    policy = jnp.sum(
        lax.all_to_all(
            by_owner.reshape(group_count, BPD, CO), "seq", split_axis=0, concat_axis=0, tiled=True
        ),
        axis=0,
    )
    return (decoded, policy)


def solution(mesh):
    placed = (
        P(("roll", "seq"), None),
        P(("roll", "seq"), None),
        P(("roll", "seq"), None),
        P(),
        P(),
        P(),
        P("seq", None, None, None),
        P("roll"),
        P("roll"),
    )
    return jax.shard_map(
        local,
        mesh=mesh,
        in_specs=placed,
        out_specs=(P(("roll", "seq"), None, None, None, None), P(("roll", "seq"), None)),
        check_vma=False,
    )
```

```python
import math

import jax
import numpy as np
import jax.numpy as jnp
from jax import lax
from jax.experimental import pallas as pl
from jax.experimental.pallas import tpu as pltpu
from jax.sharding import PartitionSpec as P

H = 24
HD = 128
LC = 16
CO = 512
S_DEV = 256
RT = 4
WT = 32
TR = 2
BPD = 2
FT = 2
RL = 8
COLS = 64
QUERY_BLOCK = 512


def shifted(array, axis, by):
    length = lax.axis_size(axis)
    pairs = [(i, i + by) for i in range(length) if 0 <= i + by < length]
    return lax.ppermute(array, axis, pairs)


def swapped(array, axis, bit):
    return lax.ppermute(array, axis, [(i, i ^ 1 << bit) for i in range(lax.axis_size(axis))])


def butterfly_sum(array, axis):
    length = lax.axis_size(axis)
    bit = 0
    while (1 << bit) < length:
        array = array + swapped(array, axis, bit)
        bit += 1
    return array


def halo_tables(tile_count):
    positions, halves = [], []
    for tile in range(tile_count):
        lower = 0 if tile % TR == 0 else 1
        earlier = tile - TR if tile >= TR else 0
        diagonal = (tile - TR) ^ 1 if tile >= TR else 0
        pos, half = [], []
        for src in (earlier, tile):
            for q in range(4):
                pos += [4 * src + q, 4 * src + q]
                half += [0, 1]
        for src in (diagonal, tile ^ 1):
            for f in range(FT):
                pos.append(4 * src + 2 * f + lower)
                half.append(lower)
        positions.append(pos)
        halves.append(half)
    return np.array(positions, np.int32), np.array(halves, np.int32)


def exchange_sum(blocks, axis, my_index):
    length = lax.axis_size(axis)
    total = lax.dynamic_index_in_dim(blocks, my_index, 0, keepdims=False)
    for step in range(1, length):
        piece = lax.dynamic_index_in_dim(blocks, (my_index + step) % length, 0, keepdims=False)
        total = total + lax.ppermute(
            piece, axis, [(i, (i + step) % length) for i in range(length)]
        )
    return total


def slot_operand(queries, keys_in, values_in, slot, group_count):
    width = group_count * HD

    def kernel(q_ref, k_ref, v_ref, out_ref):
        for part, src in enumerate((q_ref, k_ref, v_ref)):
            for group in range(group_count):
                out_ref[group, part] = src[:, group * HD : (group + 1) * HD]

    block = pl.BlockSpec((S_DEV, width), lambda i: (0, slot))
    return pl.pallas_call(
        kernel,
        grid=(1,),
        out_shape=jax.ShapeDtypeStruct((group_count, 3, S_DEV, HD), queries.dtype),
        in_specs=[block] * 3,
        out_specs=pl.BlockSpec((group_count, 3, S_DEV, HD), lambda i: (0, 0, 0, 0)),
    )(queries, keys_in, values_in)


def head_attention(query, key, value):
    length = query.shape[0]
    score_scale = 1.0 / math.sqrt(query.shape[1])
    query_blocks = query.reshape(length // QUERY_BLOCK, QUERY_BLOCK, query.shape[1])

    def one_block(query_part):
        scores = jnp.dot(query_part, key.T, preferred_element_type=jnp.float32) * score_scale
        expo = jnp.exp(scores - jnp.max(scores, axis=-1, keepdims=True))
        totals = jnp.sum(expo, axis=-1, keepdims=True)
        mixed = jnp.dot(expo.astype(jnp.bfloat16), value, preferred_element_type=jnp.float32)
        return (mixed / totals).astype(jnp.bfloat16)

    return lax.map(one_block, query_blocks).reshape(length, query.shape[1])


def window_columns(volume):
    frame_count = volume.shape[0] - 2
    row_count = volume.shape[1] - 2
    col_count = volume.shape[2] - 2
    pieces = [
        volume[a : a + frame_count, b : b + row_count, c : c + col_count]
        for a in range(3)
        for b in range(3)
        for c in range(3)
    ]
    return jnp.concatenate(pieces, axis=-1).reshape(
        frame_count * row_count * col_count, 27 * volume.shape[3]
    )


def local(
    queries,
    keys_in,
    values_in,
    latent_proj,
    conv_weight,
    conv_bias,
    pool_weight,
    tile_block,
    owner_slot,
):
    group_count = lax.axis_size("seq")
    my_index = lax.axis_index("seq")
    seq_len = S_DEV * group_count
    heads_dev = H // group_count
    quarter = S_DEV // 4

    partial = None
    for slot in range(heads_dev):
        stacked = slot_operand(queries, keys_in, values_in, slot, group_count)
        gathered = lax.all_to_all(stacked, "seq", split_axis=0, concat_axis=0, tiled=True)
        head_out = head_attention(
            *(gathered[:, part].reshape(seq_len, HD) for part in range(3))
        )
        proj_rows = lax.dynamic_slice_in_dim(latent_proj, (slot * group_count + my_index) * HD, HD, 0)
        term = jnp.dot(head_out, proj_rows, preferred_element_type=jnp.float32)
        partial = term if partial is None else partial + term

    positions, halves = halo_tables(group_count)
    picks = jnp.sum(
        jnp.where(positions[..., None] == np.arange(4 * group_count), tile_block, 0), axis=-1
    )
    half_pieces = partial.reshape(8 * group_count, quarter // 4, 8 * LC)
    outgoing = half_pieces[picks * 2 + halves].reshape(group_count, -1, 8 * LC)
    returned = lax.all_to_all(outgoing, "seq", split_axis=0, concat_axis=0, tiled=True)
    tokens = jnp.sum(returned, axis=0).reshape(-1, 4 * LC).astype(jnp.bfloat16)
    band_row = my_index % TR
    upper_band = band_row == 0
    has_earlier = my_index >= TR

    def to_tile(flat):
        return (
            flat.reshape(FT, RT, WT, 2, 2, LC).transpose(0, 1, 3, 2, 4, 5).reshape(FT, RL, COLS * LC)
        )

    def to_row(flat):
        rows = flat.reshape(FT, WT, 2, 2 * LC)
        return jnp.where(upper_band, rows[:, :, 0], rows[:, :, 1]).reshape(FT, 1, COLS * LC)

    earlier = jnp.where(has_earlier, to_tile(tokens[:S_DEV]), jnp.zeros((), jnp.bfloat16))
    tile_latent = to_tile(tokens[S_DEV : 2 * S_DEV])
    halo_len = FT * WT
    diagonal = jnp.where(
        has_earlier, to_row(tokens[2 * S_DEV : 2 * S_DEV + halo_len]), jnp.zeros((), jnp.bfloat16)
    )
    beside = to_row(tokens[2 * S_DEV + halo_len :])
    extended = jnp.concatenate([earlier, tile_latent], axis=0)
    incoming = jnp.concatenate([diagonal, beside], axis=0)
    above = jnp.where(upper_band, jnp.zeros_like(incoming), incoming)
    below = jnp.where(upper_band, incoming, jnp.zeros_like(incoming))
    volume = jnp.concatenate([above, extended, below], axis=1).reshape(FT + 2, RL + 2, COLS, LC)
    volume = jnp.pad(volume, ((0, 0), (0, 0), (1, 1), (0, 0)))
    kernel = conv_weight.reshape(3, 3, 3, LC, CO)
    pre_act = lax.conv_general_dilated(
        volume[None],
        kernel,
        window_strides=(1, 1, 1),
        padding="VALID",
        dimension_numbers=("NDHWC", "DHWIO", "NDHWC"),
        preferred_element_type=jnp.float32,
    )[0] + conv_bias
    decoded = pre_act.astype(jnp.bfloat16).reshape(1, FT, RL, COLS, CO)
    block_count = BPD * group_count
    band_voxels = group_count // TR * FT * TR * RL * (COLS // block_count)
    weighted = jax.nn.silu(pre_act).reshape(FT, RL, COLS, CO) * pool_weight[0][..., None]
    pooled_term = jnp.sum(weighted, axis=(0, 1)).reshape(block_count, COLS // block_count, CO).sum(
        axis=1
    ) / math.sqrt(band_voxels)
    slots = jnp.arange(block_count, dtype=jnp.int32)
    chooser = (owner_slot[None, :] == slots[:, None]).astype(jnp.float32)
    by_owner = jnp.dot(
        chooser, pooled_term, precision=lax.Precision.HIGHEST, preferred_element_type=jnp.float32
    )
    policy = jnp.sum(
        lax.all_to_all(
            by_owner.reshape(group_count, BPD, CO), "seq", split_axis=0, concat_axis=0, tiled=True
        ),
        axis=0,
    )
    return (decoded, policy)


def solution(mesh):
    placed = (
        P(("roll", "seq"), None),
        P(("roll", "seq"), None),
        P(("roll", "seq"), None),
        P(),
        P(),
        P(),
        P("seq", None, None, None),
        P("roll"),
        P("roll"),
    )
    return jax.shard_map(
        local,
        mesh=mesh,
        in_specs=placed,
        out_specs=(P(("roll", "seq"), None, None, None, None), P(("roll", "seq"), None)),
        check_vma=False,
    )
```

```python
import math

import jax
import numpy as np
import jax.numpy as jnp
from jax import lax
from jax.experimental import pallas as pl
from jax.experimental.pallas import tpu as pltpu
from jax.sharding import PartitionSpec as P

H = 24
HD = 128
LC = 16
CO = 512
S_DEV = 256
RT = 4
WT = 32
TR = 2
BPD = 2
FT = 2
RL = 8
COLS = 64
QUERY_BLOCK = 256


def shifted(array, axis, by):
    length = lax.axis_size(axis)
    pairs = [(i, i + by) for i in range(length) if 0 <= i + by < length]
    return lax.ppermute(array, axis, pairs)


def swapped(array, axis, bit):
    return lax.ppermute(array, axis, [(i, i ^ 1 << bit) for i in range(lax.axis_size(axis))])


def butterfly_sum(array, axis):
    length = lax.axis_size(axis)
    bit = 0
    while (1 << bit) < length:
        array = array + swapped(array, axis, bit)
        bit += 1
    return array


def halo_tables(tile_count):
    positions, halves = [], []
    for tile in range(tile_count):
        lower = 0 if tile % TR == 0 else 1
        earlier = tile - TR if tile >= TR else 0
        diagonal = (tile - TR) ^ 1 if tile >= TR else 0
        pos, half = [], []
        for src in (earlier, tile):
            for q in range(4):
                pos += [4 * src + q, 4 * src + q]
                half += [0, 1]
        for src in (diagonal, tile ^ 1):
            for f in range(FT):
                pos.append(4 * src + 2 * f + lower)
                half.append(lower)
        positions.append(pos)
        halves.append(half)
    return np.array(positions, np.int32), np.array(halves, np.int32)


def exchange_sum(blocks, axis, my_index):
    length = lax.axis_size(axis)
    total = lax.dynamic_index_in_dim(blocks, my_index, 0, keepdims=False)
    for step in range(1, length):
        piece = lax.dynamic_index_in_dim(blocks, (my_index + step) % length, 0, keepdims=False)
        total = total + lax.ppermute(
            piece, axis, [(i, (i + step) % length) for i in range(length)]
        )
    return total


def slot_operand(queries, keys_in, values_in, slot, group_count):
    width = group_count * HD

    def kernel(q_ref, k_ref, v_ref, out_ref):
        for part, src in enumerate((q_ref, k_ref, v_ref)):
            for group in range(group_count):
                out_ref[group, part] = src[:, group * HD : (group + 1) * HD]

    block = pl.BlockSpec((S_DEV, width), lambda i: (0, slot))
    return pl.pallas_call(
        kernel,
        grid=(1,),
        out_shape=jax.ShapeDtypeStruct((group_count, 3, S_DEV, HD), queries.dtype),
        in_specs=[block] * 3,
        out_specs=pl.BlockSpec((group_count, 3, S_DEV, HD), lambda i: (0, 0, 0, 0)),
    )(queries, keys_in, values_in)


def head_attention(query, key, value):
    length, width = query.shape
    score_scale = 1.0 / math.sqrt(width)

    def kernel(q_ref, k_ref, v_ref, out_ref):
        scores = (
            lax.dot_general(
                q_ref[...],
                k_ref[...],
                (((1,), (1,)), ((), ())),
                preferred_element_type=jnp.float32,
            )
            * score_scale
        )
        expo = jnp.exp(scores - jnp.max(scores, axis=-1, keepdims=True))
        totals = jnp.sum(expo, axis=-1, keepdims=True)
        mixed = jnp.dot(expo.astype(jnp.bfloat16), v_ref[...], preferred_element_type=jnp.float32)
        out_ref[...] = (mixed / totals).astype(out_ref.dtype)

    whole = pl.BlockSpec((length, width), lambda i: (0, 0))
    rows = pl.BlockSpec((QUERY_BLOCK, width), lambda i: (i, 0))
    return pl.pallas_call(
        kernel,
        grid=(length // QUERY_BLOCK,),
        out_shape=jax.ShapeDtypeStruct((length, width), query.dtype),
        in_specs=[rows, whole, whole],
        out_specs=rows,
    )(query, key, value)


def window_columns(volume):
    frame_count = volume.shape[0] - 2
    row_count = volume.shape[1] - 2
    col_count = volume.shape[2] - 2
    pieces = [
        volume[a : a + frame_count, b : b + row_count, c : c + col_count]
        for a in range(3)
        for b in range(3)
        for c in range(3)
    ]
    return jnp.concatenate(pieces, axis=-1).reshape(
        frame_count * row_count * col_count, 27 * volume.shape[3]
    )


def local(
    queries,
    keys_in,
    values_in,
    latent_proj,
    conv_weight,
    conv_bias,
    pool_weight,
    tile_block,
    owner_slot,
):
    group_count = lax.axis_size("seq")
    my_index = lax.axis_index("seq")
    seq_len = S_DEV * group_count
    heads_dev = H // group_count
    quarter = S_DEV // 4

    partial = None
    for slot in range(heads_dev):
        stacked = slot_operand(queries, keys_in, values_in, slot, group_count)
        gathered = lax.all_to_all(stacked, "seq", split_axis=0, concat_axis=0, tiled=True)
        head_out = head_attention(
            *(gathered[:, part].reshape(seq_len, HD) for part in range(3))
        )
        proj_rows = lax.dynamic_slice_in_dim(latent_proj, (slot * group_count + my_index) * HD, HD, 0)
        term = jnp.dot(head_out, proj_rows, preferred_element_type=jnp.float32)
        partial = term if partial is None else partial + term

    positions, halves = halo_tables(group_count)
    picks = jnp.sum(
        jnp.where(positions[..., None] == np.arange(4 * group_count), tile_block, 0), axis=-1
    )
    half_pieces = partial.reshape(8 * group_count, quarter // 4, 8 * LC)
    outgoing = half_pieces[picks * 2 + halves].reshape(group_count, -1, 8 * LC)
    returned = lax.all_to_all(outgoing, "seq", split_axis=0, concat_axis=0, tiled=True)
    tokens = jnp.sum(returned, axis=0).reshape(-1, 4 * LC).astype(jnp.bfloat16)
    band_row = my_index % TR
    upper_band = band_row == 0
    has_earlier = my_index >= TR

    def to_tile(flat):
        return (
            flat.reshape(FT, RT, WT, 2, 2, LC).transpose(0, 1, 3, 2, 4, 5).reshape(FT, RL, COLS * LC)
        )

    def to_row(flat):
        rows = flat.reshape(FT, WT, 2, 2 * LC)
        return jnp.where(upper_band, rows[:, :, 0], rows[:, :, 1]).reshape(FT, 1, COLS * LC)

    earlier = jnp.where(has_earlier, to_tile(tokens[:S_DEV]), jnp.zeros((), jnp.bfloat16))
    tile_latent = to_tile(tokens[S_DEV : 2 * S_DEV])
    halo_len = FT * WT
    diagonal = jnp.where(
        has_earlier, to_row(tokens[2 * S_DEV : 2 * S_DEV + halo_len]), jnp.zeros((), jnp.bfloat16)
    )
    beside = to_row(tokens[2 * S_DEV + halo_len :])
    extended = jnp.concatenate([earlier, tile_latent], axis=0)
    incoming = jnp.concatenate([diagonal, beside], axis=0)
    above = jnp.where(upper_band, jnp.zeros_like(incoming), incoming)
    below = jnp.where(upper_band, incoming, jnp.zeros_like(incoming))
    volume = jnp.concatenate([above, extended, below], axis=1).reshape(FT + 2, RL + 2, COLS, LC)
    volume = jnp.pad(volume, ((0, 0), (0, 0), (1, 1), (0, 0)))
    kernel = conv_weight.reshape(3, 3, 3, LC, CO)
    pre_act = lax.conv_general_dilated(
        volume[None],
        kernel,
        window_strides=(1, 1, 1),
        padding="VALID",
        dimension_numbers=("NDHWC", "DHWIO", "NDHWC"),
        preferred_element_type=jnp.float32,
    )[0] + conv_bias
    decoded = pre_act.astype(jnp.bfloat16).reshape(1, FT, RL, COLS, CO)
    block_count = BPD * group_count
    band_voxels = group_count // TR * FT * TR * RL * (COLS // block_count)
    weighted = jax.nn.silu(pre_act).reshape(FT, RL, COLS, CO) * pool_weight[0][..., None]
    pooled_term = jnp.sum(weighted, axis=(0, 1)).reshape(block_count, COLS // block_count, CO).sum(
        axis=1
    ) / math.sqrt(band_voxels)
    slots = jnp.arange(block_count, dtype=jnp.int32)
    chooser = (owner_slot[None, :] == slots[:, None]).astype(jnp.float32)
    by_owner = jnp.dot(
        chooser, pooled_term, precision=lax.Precision.HIGHEST, preferred_element_type=jnp.float32
    )
    policy = jnp.sum(
        lax.all_to_all(
            by_owner.reshape(group_count, BPD, CO), "seq", split_axis=0, concat_axis=0, tiled=True
        ),
        axis=0,
    )
    return (decoded, policy)


def solution(mesh):
    placed = (
        P(("roll", "seq"), None),
        P(("roll", "seq"), None),
        P(("roll", "seq"), None),
        P(),
        P(),
        P(),
        P("seq", None, None, None),
        P("roll"),
        P("roll"),
    )
    return jax.shard_map(
        local,
        mesh=mesh,
        in_specs=placed,
        out_specs=(P(("roll", "seq"), None, None, None, None), P(("roll", "seq"), None)),
        check_vma=False,
    )
```

```python
import math

import jax
import numpy as np
import jax.numpy as jnp
from jax import lax
from jax.experimental import pallas as pl
from jax.experimental.pallas import tpu as pltpu
from jax.sharding import PartitionSpec as P

H = 24
HD = 128
LC = 16
CO = 512
S_DEV = 256
RT = 4
WT = 32
TR = 2
BPD = 2
FT = 2
RL = 8
COLS = 64
QUERY_BLOCK = 1024


def shifted(array, axis, by):
    length = lax.axis_size(axis)
    pairs = [(i, i + by) for i in range(length) if 0 <= i + by < length]
    return lax.ppermute(array, axis, pairs)


def swapped(array, axis, bit):
    return lax.ppermute(array, axis, [(i, i ^ 1 << bit) for i in range(lax.axis_size(axis))])


def butterfly_sum(array, axis):
    length = lax.axis_size(axis)
    bit = 0
    while (1 << bit) < length:
        array = array + swapped(array, axis, bit)
        bit += 1
    return array


def halo_tables(tile_count):
    positions, halves = [], []
    for tile in range(tile_count):
        lower = 0 if tile % TR == 0 else 1
        earlier = tile - TR if tile >= TR else 0
        diagonal = (tile - TR) ^ 1 if tile >= TR else 0
        pos, half = [], []
        for src in (earlier, tile):
            for q in range(4):
                pos += [4 * src + q, 4 * src + q]
                half += [0, 1]
        for src in (diagonal, tile ^ 1):
            for f in range(FT):
                pos.append(4 * src + 2 * f + lower)
                half.append(lower)
        positions.append(pos)
        halves.append(half)
    return np.array(positions, np.int32), np.array(halves, np.int32)


def exchange_sum(blocks, axis, my_index):
    length = lax.axis_size(axis)
    total = lax.dynamic_index_in_dim(blocks, my_index, 0, keepdims=False)
    for step in range(1, length):
        piece = lax.dynamic_index_in_dim(blocks, (my_index + step) % length, 0, keepdims=False)
        total = total + lax.ppermute(
            piece, axis, [(i, (i + step) % length) for i in range(length)]
        )
    return total


def slot_operand(queries, keys_in, values_in, slot, group_count):
    width = group_count * HD

    def kernel(q_ref, k_ref, v_ref, out_ref):
        for part, src in enumerate((q_ref, k_ref, v_ref)):
            for group in range(group_count):
                out_ref[group, part] = src[:, group * HD : (group + 1) * HD]

    block = pl.BlockSpec((S_DEV, width), lambda i: (0, slot))
    return pl.pallas_call(
        kernel,
        grid=(1,),
        out_shape=jax.ShapeDtypeStruct((group_count, 3, S_DEV, HD), queries.dtype),
        in_specs=[block] * 3,
        out_specs=pl.BlockSpec((group_count, 3, S_DEV, HD), lambda i: (0, 0, 0, 0)),
    )(queries, keys_in, values_in)


def head_attention(query, key, value):
    length = query.shape[0]
    score_scale = 1.0 / math.sqrt(query.shape[1])
    query_blocks = query.reshape(length // QUERY_BLOCK, QUERY_BLOCK, query.shape[1])

    def one_block(query_part):
        scores = jnp.dot(query_part, key.T, preferred_element_type=jnp.float32) * score_scale
        expo = jnp.exp(scores - jnp.max(scores, axis=-1, keepdims=True))
        totals = jnp.sum(expo, axis=-1, keepdims=True)
        mixed = jnp.dot(expo.astype(jnp.bfloat16), value, preferred_element_type=jnp.float32)
        return (mixed / totals).astype(jnp.bfloat16)

    return lax.map(one_block, query_blocks).reshape(length, query.shape[1])


def window_columns(volume):
    frame_count = volume.shape[0] - 2
    row_count = volume.shape[1] - 2
    col_count = volume.shape[2] - 2
    pieces = [
        volume[a : a + frame_count, b : b + row_count, c : c + col_count]
        for a in range(3)
        for b in range(3)
        for c in range(3)
    ]
    return jnp.concatenate(pieces, axis=-1).reshape(
        frame_count * row_count * col_count, 27 * volume.shape[3]
    )


def local(
    queries,
    keys_in,
    values_in,
    latent_proj,
    conv_weight,
    conv_bias,
    pool_weight,
    tile_block,
    owner_slot,
):
    group_count = lax.axis_size("seq")
    my_index = lax.axis_index("seq")
    seq_len = S_DEV * group_count
    heads_dev = H // group_count
    quarter = S_DEV // 4

    partial = None
    for slot in range(heads_dev):
        stacked = slot_operand(queries, keys_in, values_in, slot, group_count)
        gathered = lax.all_to_all(stacked, "seq", split_axis=0, concat_axis=0, tiled=True)
        head_out = head_attention(
            *(gathered[:, part].reshape(seq_len, HD) for part in range(3))
        )
        proj_rows = lax.dynamic_slice_in_dim(latent_proj, (slot * group_count + my_index) * HD, HD, 0)
        term = jnp.dot(head_out, proj_rows, preferred_element_type=jnp.float32)
        partial = term if partial is None else partial + term

    positions, halves = halo_tables(group_count)
    picks = jnp.sum(
        jnp.where(positions[..., None] == np.arange(4 * group_count), tile_block, 0), axis=-1
    )
    half_pieces = partial.reshape(8 * group_count, quarter // 4, 8 * LC)
    outgoing = half_pieces[picks * 2 + halves].reshape(group_count, -1, 8 * LC)
    returned = lax.all_to_all(outgoing, "seq", split_axis=0, concat_axis=0, tiled=True)
    tokens = jnp.sum(returned, axis=0).reshape(-1, 4 * LC).astype(jnp.bfloat16)
    band_row = my_index % TR
    upper_band = band_row == 0
    has_earlier = my_index >= TR

    def to_tile(flat):
        return (
            flat.reshape(FT, RT, WT, 2, 2, LC).transpose(0, 1, 3, 2, 4, 5).reshape(FT, RL, COLS * LC)
        )

    def to_row(flat):
        rows = flat.reshape(FT, WT, 2, 2 * LC)
        return jnp.where(upper_band, rows[:, :, 0], rows[:, :, 1]).reshape(FT, 1, COLS * LC)

    earlier = jnp.where(has_earlier, to_tile(tokens[:S_DEV]), jnp.zeros((), jnp.bfloat16))
    tile_latent = to_tile(tokens[S_DEV : 2 * S_DEV])
    halo_len = FT * WT
    diagonal = jnp.where(
        has_earlier, to_row(tokens[2 * S_DEV : 2 * S_DEV + halo_len]), jnp.zeros((), jnp.bfloat16)
    )
    beside = to_row(tokens[2 * S_DEV + halo_len :])
    extended = jnp.concatenate([earlier, tile_latent], axis=0)
    incoming = jnp.concatenate([diagonal, beside], axis=0)
    above = jnp.where(upper_band, jnp.zeros_like(incoming), incoming)
    below = jnp.where(upper_band, incoming, jnp.zeros_like(incoming))
    volume = jnp.concatenate([above, extended, below], axis=1).reshape(FT + 2, RL + 2, COLS, LC)
    volume = jnp.pad(volume, ((0, 0), (0, 0), (1, 1), (0, 0)))
    kernel = conv_weight.reshape(3, 3, 3, LC, CO)
    pre_act = lax.conv_general_dilated(
        volume[None],
        kernel,
        window_strides=(1, 1, 1),
        padding="VALID",
        dimension_numbers=("NDHWC", "DHWIO", "NDHWC"),
        preferred_element_type=jnp.float32,
    )[0] + conv_bias
    decoded = pre_act.astype(jnp.bfloat16).reshape(1, FT, RL, COLS, CO)
    block_count = BPD * group_count
    band_voxels = group_count // TR * FT * TR * RL * (COLS // block_count)
    weighted = jax.nn.silu(pre_act).reshape(FT, RL, COLS, CO) * pool_weight[0][..., None]
    pooled_term = jnp.sum(weighted, axis=(0, 1)).reshape(block_count, COLS // block_count, CO).sum(
        axis=1
    ) / math.sqrt(band_voxels)
    slots = jnp.arange(block_count, dtype=jnp.int32)
    chooser = (owner_slot[None, :] == slots[:, None]).astype(jnp.float32)
    by_owner = jnp.dot(
        chooser, pooled_term, precision=lax.Precision.HIGHEST, preferred_element_type=jnp.float32
    )
    policy = jnp.sum(
        lax.all_to_all(
            by_owner.reshape(group_count, BPD, CO), "seq", split_axis=0, concat_axis=0, tiled=True
        ),
        axis=0,
    )
    return (decoded, policy)


def solution(mesh):
    placed = (
        P(("roll", "seq"), None),
        P(("roll", "seq"), None),
        P(("roll", "seq"), None),
        P(),
        P(),
        P(),
        P("seq", None, None, None),
        P("roll"),
        P("roll"),
    )
    return jax.shard_map(
        local,
        mesh=mesh,
        in_specs=placed,
        out_specs=(P(("roll", "seq"), None, None, None, None), P(("roll", "seq"), None)),
        check_vma=False,
    )
```

```python
import math

import jax
import numpy as np
import jax.numpy as jnp
from jax import lax
from jax.experimental import pallas as pl
from jax.experimental.pallas import tpu as pltpu
from jax.sharding import PartitionSpec as P

H = 24
HD = 128
LC = 16
CO = 512
S_DEV = 256
RT = 4
WT = 32
TR = 2
BPD = 2
FT = 2
RL = 8
COLS = 64
QUERY_BLOCK = 1024


def shifted(array, axis, by):
    length = lax.axis_size(axis)
    pairs = [(i, i + by) for i in range(length) if 0 <= i + by < length]
    return lax.ppermute(array, axis, pairs)


def swapped(array, axis, bit):
    return lax.ppermute(array, axis, [(i, i ^ 1 << bit) for i in range(lax.axis_size(axis))])


def butterfly_sum(array, axis):
    length = lax.axis_size(axis)
    bit = 0
    while (1 << bit) < length:
        array = array + swapped(array, axis, bit)
        bit += 1
    return array


def halo_tables(tile_count):
    positions, halves = [], []
    for tile in range(tile_count):
        lower = 0 if tile % TR == 0 else 1
        diagonal = (tile - TR) ^ 1 if tile >= TR else 0
        pos, half = [], []
        for src in (tile,):
            for q in range(4):
                pos += [4 * src + q, 4 * src + q]
                half += [0, 1]
        for src in (diagonal, tile ^ 1):
            for f in range(FT):
                pos.append(4 * src + 2 * f + lower)
                half.append(lower)
        positions.append(pos)
        halves.append(half)
    return np.array(positions, np.int32), np.array(halves, np.int32)


def exchange_sum(blocks, axis, my_index):
    length = lax.axis_size(axis)
    total = lax.dynamic_index_in_dim(blocks, my_index, 0, keepdims=False)
    for step in range(1, length):
        piece = lax.dynamic_index_in_dim(blocks, (my_index + step) % length, 0, keepdims=False)
        total = total + lax.ppermute(
            piece, axis, [(i, (i + step) % length) for i in range(length)]
        )
    return total


def slot_operand(queries, keys_in, values_in, slot, group_count):
    width = group_count * HD

    def kernel(q_ref, k_ref, v_ref, out_ref):
        for part, src in enumerate((q_ref, k_ref, v_ref)):
            for group in range(group_count):
                out_ref[group, part] = src[:, group * HD : (group + 1) * HD]

    block = pl.BlockSpec((S_DEV, width), lambda i: (0, slot))
    return pl.pallas_call(
        kernel,
        grid=(1,),
        out_shape=jax.ShapeDtypeStruct((group_count, 3, S_DEV, HD), queries.dtype),
        in_specs=[block] * 3,
        out_specs=pl.BlockSpec((group_count, 3, S_DEV, HD), lambda i: (0, 0, 0, 0)),
    )(queries, keys_in, values_in)


def head_attention(query, key, value):
    length = query.shape[0]
    score_scale = 1.0 / math.sqrt(query.shape[1])
    query_blocks = query.reshape(length // QUERY_BLOCK, QUERY_BLOCK, query.shape[1])

    def one_block(query_part):
        scores = jnp.dot(query_part, key.T, preferred_element_type=jnp.float32) * score_scale
        expo = jnp.exp(scores - jnp.max(scores, axis=-1, keepdims=True))
        totals = jnp.sum(expo, axis=-1, keepdims=True)
        mixed = jnp.dot(expo.astype(jnp.bfloat16), value, preferred_element_type=jnp.float32)
        return (mixed / totals).astype(jnp.bfloat16)

    return lax.map(one_block, query_blocks).reshape(length, query.shape[1])


def window_columns(volume):
    frame_count = volume.shape[0] - 2
    row_count = volume.shape[1] - 2
    col_count = volume.shape[2] - 2
    pieces = [
        volume[a : a + frame_count, b : b + row_count, c : c + col_count]
        for a in range(3)
        for b in range(3)
        for c in range(3)
    ]
    return jnp.concatenate(pieces, axis=-1).reshape(
        frame_count * row_count * col_count, 27 * volume.shape[3]
    )


def local(
    queries,
    keys_in,
    values_in,
    latent_proj,
    conv_weight,
    conv_bias,
    pool_weight,
    tile_block,
    owner_slot,
):
    group_count = lax.axis_size("seq")
    my_index = lax.axis_index("seq")
    seq_len = S_DEV * group_count
    heads_dev = H // group_count
    quarter = S_DEV // 4

    partial = None
    for slot in range(heads_dev):
        stacked = slot_operand(queries, keys_in, values_in, slot, group_count)
        gathered = lax.all_to_all(stacked, "seq", split_axis=0, concat_axis=0, tiled=True)
        head_out = head_attention(
            *(gathered[:, part].reshape(seq_len, HD) for part in range(3))
        )
        proj_rows = lax.dynamic_slice_in_dim(latent_proj, (slot * group_count + my_index) * HD, HD, 0)
        term = jnp.dot(head_out, proj_rows, preferred_element_type=jnp.float32)
        partial = term if partial is None else partial + term

    positions, halves = halo_tables(group_count)
    picks = jnp.sum(
        jnp.where(positions[..., None] == np.arange(4 * group_count), tile_block, 0), axis=-1
    )
    half_pieces = partial.reshape(8 * group_count, quarter // 4, 8 * LC)
    outgoing = half_pieces[picks * 2 + halves].reshape(group_count, -1, 8 * LC)
    returned = lax.all_to_all(outgoing, "seq", split_axis=0, concat_axis=0, tiled=True)
    tokens = jnp.sum(returned, axis=0).reshape(-1, 4 * LC).astype(jnp.bfloat16)
    band_row = my_index % TR
    upper_band = band_row == 0
    has_earlier = my_index >= TR

    def to_tile(flat):
        return (
            flat.reshape(FT, RT, WT, 2, 2, LC).transpose(0, 1, 3, 2, 4, 5).reshape(FT, RL, COLS * LC)
        )

    def to_row(flat):
        rows = flat.reshape(FT, WT, 2, 2 * LC)
        return jnp.where(upper_band, rows[:, :, 0], rows[:, :, 1]).reshape(FT, 1, COLS * LC)

    tile_latent = to_tile(tokens[:S_DEV])
    earlier = shifted(tile_latent, "seq", TR)
    halo_len = FT * WT
    diagonal = jnp.where(
        has_earlier, to_row(tokens[S_DEV : S_DEV + halo_len]), jnp.zeros((), jnp.bfloat16)
    )
    beside = to_row(tokens[S_DEV + halo_len :])
    extended = jnp.concatenate([earlier, tile_latent], axis=0)
    incoming = jnp.concatenate([diagonal, beside], axis=0)
    above = jnp.where(upper_band, jnp.zeros_like(incoming), incoming)
    below = jnp.where(upper_band, incoming, jnp.zeros_like(incoming))
    volume = jnp.concatenate([above, extended, below], axis=1).reshape(FT + 2, RL + 2, COLS, LC)
    volume = jnp.pad(volume, ((0, 0), (0, 0), (1, 1), (0, 0)))
    kernel = conv_weight.reshape(3, 3, 3, LC, CO)
    pre_act = lax.conv_general_dilated(
        volume[None],
        kernel,
        window_strides=(1, 1, 1),
        padding="VALID",
        dimension_numbers=("NDHWC", "DHWIO", "NDHWC"),
        preferred_element_type=jnp.float32,
    )[0] + conv_bias
    decoded = pre_act.astype(jnp.bfloat16).reshape(1, FT, RL, COLS, CO)
    block_count = BPD * group_count
    band_voxels = group_count // TR * FT * TR * RL * (COLS // block_count)
    weighted = jax.nn.silu(pre_act).reshape(FT, RL, COLS, CO) * pool_weight[0][..., None]
    pooled_term = jnp.sum(weighted, axis=(0, 1)).reshape(block_count, COLS // block_count, CO).sum(
        axis=1
    ) / math.sqrt(band_voxels)
    slots = jnp.arange(block_count, dtype=jnp.int32)
    chooser = (owner_slot[None, :] == slots[:, None]).astype(jnp.float32)
    by_owner = jnp.dot(
        chooser, pooled_term, precision=lax.Precision.HIGHEST, preferred_element_type=jnp.float32
    )
    policy = jnp.sum(
        lax.all_to_all(
            by_owner.reshape(group_count, BPD, CO), "seq", split_axis=0, concat_axis=0, tiled=True
        ),
        axis=0,
    )
    return (decoded, policy)


def solution(mesh):
    placed = (
        P(("roll", "seq"), None),
        P(("roll", "seq"), None),
        P(("roll", "seq"), None),
        P(),
        P(),
        P(),
        P("seq", None, None, None),
        P("roll"),
        P("roll"),
    )
    return jax.shard_map(
        local,
        mesh=mesh,
        in_specs=placed,
        out_specs=(P(("roll", "seq"), None, None, None, None), P(("roll", "seq"), None)),
        check_vma=False,
    )
```

```python
import math

import jax
import numpy as np
import jax.numpy as jnp
from jax import lax
from jax.experimental import pallas as pl
from jax.experimental.pallas import tpu as pltpu
from jax.sharding import PartitionSpec as P

H = 24
HD = 128
LC = 16
CO = 512
S_DEV = 256
RT = 4
WT = 32
TR = 2
BPD = 2
FT = 2
RL = 8
COLS = 64
QUERY_BLOCK = 1024


def shifted(array, axis, by):
    length = lax.axis_size(axis)
    pairs = [(i, i + by) for i in range(length) if 0 <= i + by < length]
    return lax.ppermute(array, axis, pairs)


def swapped(array, axis, bit):
    return lax.ppermute(array, axis, [(i, i ^ 1 << bit) for i in range(lax.axis_size(axis))])


def butterfly_sum(array, axis):
    length = lax.axis_size(axis)
    bit = 0
    while (1 << bit) < length:
        array = array + swapped(array, axis, bit)
        bit += 1
    return array


def halo_tables(tile_count):
    positions, halves = [], []
    for tile in range(tile_count):
        lower = 0 if tile % TR == 0 else 1
        earlier = tile - TR if tile >= TR else 0
        diagonal = (tile - TR) ^ 1 if tile >= TR else 0
        pos, half = [], []
        for src in (earlier, tile):
            for q in range(4):
                pos += [4 * src + q, 4 * src + q]
                half += [0, 1]
        for src in (diagonal, tile ^ 1):
            for f in range(FT):
                pos.append(4 * src + 2 * f + lower)
                half.append(lower)
        positions.append(pos)
        halves.append(half)
    return np.array(positions, np.int32), np.array(halves, np.int32)


def exchange_sum(blocks, axis, my_index):
    length = lax.axis_size(axis)
    total = lax.dynamic_index_in_dim(blocks, my_index, 0, keepdims=False)
    for step in range(1, length):
        piece = lax.dynamic_index_in_dim(blocks, (my_index + step) % length, 0, keepdims=False)
        total = total + lax.ppermute(
            piece, axis, [(i, (i + step) % length) for i in range(length)]
        )
    return total


def slot_operand(queries, keys_in, values_in, slot, group_count):
    width = group_count * HD

    def kernel(q_ref, k_ref, v_ref, out_ref):
        for part, src in enumerate((q_ref, k_ref, v_ref)):
            for group in range(group_count):
                out_ref[group, part] = src[:, group * HD : (group + 1) * HD]

    block = pl.BlockSpec((S_DEV, width), lambda i: (0, slot))
    return pl.pallas_call(
        kernel,
        grid=(1,),
        out_shape=jax.ShapeDtypeStruct((group_count, 3, S_DEV, HD), queries.dtype),
        in_specs=[block] * 3,
        out_specs=pl.BlockSpec((group_count, 3, S_DEV, HD), lambda i: (0, 0, 0, 0)),
    )(queries, keys_in, values_in)


def head_attention(query, key, value):
    length = query.shape[0]
    score_scale = 1.0 / math.sqrt(query.shape[1])
    query_blocks = query.reshape(length // QUERY_BLOCK, QUERY_BLOCK, query.shape[1])

    def one_block(query_part):
        scores = jnp.dot(query_part, key.T, preferred_element_type=jnp.float32) * score_scale
        expo = jnp.exp(scores - jnp.max(scores, axis=-1, keepdims=True))
        totals = jnp.sum(expo, axis=-1, keepdims=True)
        mixed = jnp.dot(expo.astype(jnp.bfloat16), value, preferred_element_type=jnp.float32)
        return (mixed / totals).astype(jnp.bfloat16)

    return jnp.concatenate([one_block(part) for part in query_blocks], axis=0)


def window_columns(volume):
    frame_count = volume.shape[0] - 2
    row_count = volume.shape[1] - 2
    col_count = volume.shape[2] - 2
    pieces = [
        volume[a : a + frame_count, b : b + row_count, c : c + col_count]
        for a in range(3)
        for b in range(3)
        for c in range(3)
    ]
    return jnp.concatenate(pieces, axis=-1).reshape(
        frame_count * row_count * col_count, 27 * volume.shape[3]
    )


def local(
    queries,
    keys_in,
    values_in,
    latent_proj,
    conv_weight,
    conv_bias,
    pool_weight,
    tile_block,
    owner_slot,
):
    group_count = lax.axis_size("seq")
    my_index = lax.axis_index("seq")
    seq_len = S_DEV * group_count
    heads_dev = H // group_count
    quarter = S_DEV // 4

    partial = None
    for slot in range(heads_dev):
        stacked = slot_operand(queries, keys_in, values_in, slot, group_count)
        gathered = lax.all_to_all(stacked, "seq", split_axis=0, concat_axis=0, tiled=True)
        head_out = head_attention(
            *(gathered[:, part].reshape(seq_len, HD) for part in range(3))
        )
        proj_rows = lax.dynamic_slice_in_dim(latent_proj, (slot * group_count + my_index) * HD, HD, 0)
        term = jnp.dot(head_out, proj_rows, preferred_element_type=jnp.float32)
        partial = term if partial is None else partial + term

    positions, halves = halo_tables(group_count)
    picks = jnp.sum(
        jnp.where(positions[..., None] == np.arange(4 * group_count), tile_block, 0), axis=-1
    )
    half_pieces = partial.reshape(8 * group_count, quarter // 4, 8 * LC)
    outgoing = half_pieces[picks * 2 + halves].reshape(group_count, -1, 8 * LC)
    returned = lax.all_to_all(outgoing, "seq", split_axis=0, concat_axis=0, tiled=True)
    tokens = jnp.sum(returned, axis=0).reshape(-1, 4 * LC).astype(jnp.bfloat16)
    band_row = my_index % TR
    upper_band = band_row == 0
    has_earlier = my_index >= TR

    def to_tile(flat):
        return (
            flat.reshape(FT, RT, WT, 2, 2, LC).transpose(0, 1, 3, 2, 4, 5).reshape(FT, RL, COLS * LC)
        )

    def to_row(flat):
        rows = flat.reshape(FT, WT, 2, 2 * LC)
        return jnp.where(upper_band, rows[:, :, 0], rows[:, :, 1]).reshape(FT, 1, COLS * LC)

    earlier = jnp.where(has_earlier, to_tile(tokens[:S_DEV]), jnp.zeros((), jnp.bfloat16))
    tile_latent = to_tile(tokens[S_DEV : 2 * S_DEV])
    halo_len = FT * WT
    diagonal = jnp.where(
        has_earlier, to_row(tokens[2 * S_DEV : 2 * S_DEV + halo_len]), jnp.zeros((), jnp.bfloat16)
    )
    beside = to_row(tokens[2 * S_DEV + halo_len :])
    extended = jnp.concatenate([earlier, tile_latent], axis=0)
    incoming = jnp.concatenate([diagonal, beside], axis=0)
    above = jnp.where(upper_band, jnp.zeros_like(incoming), incoming)
    below = jnp.where(upper_band, incoming, jnp.zeros_like(incoming))
    volume = jnp.concatenate([above, extended, below], axis=1).reshape(FT + 2, RL + 2, COLS, LC)
    volume = jnp.pad(volume, ((0, 0), (0, 0), (1, 1), (0, 0)))
    kernel = conv_weight.reshape(3, 3, 3, LC, CO)
    pre_act = lax.conv_general_dilated(
        volume[None],
        kernel,
        window_strides=(1, 1, 1),
        padding="VALID",
        dimension_numbers=("NDHWC", "DHWIO", "NDHWC"),
        preferred_element_type=jnp.float32,
    )[0] + conv_bias
    decoded = pre_act.astype(jnp.bfloat16).reshape(1, FT, RL, COLS, CO)
    block_count = BPD * group_count
    band_voxels = group_count // TR * FT * TR * RL * (COLS // block_count)
    weighted = jax.nn.silu(pre_act).reshape(FT, RL, COLS, CO) * pool_weight[0][..., None]
    pooled_term = jnp.sum(weighted, axis=(0, 1)).reshape(block_count, COLS // block_count, CO).sum(
        axis=1
    ) / math.sqrt(band_voxels)
    slots = jnp.arange(block_count, dtype=jnp.int32)
    chooser = (owner_slot[None, :] == slots[:, None]).astype(jnp.float32)
    by_owner = jnp.dot(
        chooser, pooled_term, precision=lax.Precision.HIGHEST, preferred_element_type=jnp.float32
    )
    policy = jnp.sum(
        lax.all_to_all(
            by_owner.reshape(group_count, BPD, CO), "seq", split_axis=0, concat_axis=0, tiled=True
        ),
        axis=0,
    )
    return (decoded, policy)


def solution(mesh):
    placed = (
        P(("roll", "seq"), None),
        P(("roll", "seq"), None),
        P(("roll", "seq"), None),
        P(),
        P(),
        P(),
        P("seq", None, None, None),
        P("roll"),
        P("roll"),
    )
    return jax.shard_map(
        local,
        mesh=mesh,
        in_specs=placed,
        out_specs=(P(("roll", "seq"), None, None, None, None), P(("roll", "seq"), None)),
        check_vma=False,
    )
```
